512 devices in a mesh: grp: 8 (over x, y_lo), dom: 64 (over y_hi, z, core).
Axes of the slice: x: 4, y: 4 (y_hi: 2, y_lo: 2; y = y_hi * 2 + y_lo), z: 16, core: 2. Of those that a mesh axis runs over, the one named last changes fastest.
Arguments:
- state: float32 [56, 9, 65536], P(None, None, ('grp', 'dom')), may hold values from -6 to 6
- star: float32 [3, 9, 9, 65536], P(None, None, None, ('grp', 'dom')), may hold values from -1.75 to 1.75
- flux_own: float32 [4, 9, 9, 65536], P(None, None, None, ('grp', 'dom')), may hold values from -0.875 to 0.875
- flux_nbr: float32 [4, 9, 9, 65536], P(None, None, None, ('grp', 'dom')), may hold values from -0.875 to 0.875
- stiff: float32 [3, 56, 56], replicated, may hold values from -0.75 to 0.75
- trace: float32 [4, 21, 56], replicated, may hold values from -0.75 to 0.75
- lift: float32 [4, 56, 21], replicated, may hold values from -1.25 to 1.25
- nbr_slot: int32 [4, 65536], P(None, ('grp', 'dom')), may hold values from 0 to 511, as said below
- nbr_face: int32 [4, 65536], P(None, ('grp', 'dom')), may hold values from 0 to 3, as said below
- send_slot: int32 [196608], P(('grp', 'dom')), may hold values from 0 to 511, as said below
Outputs:
- new_state: float32 [56, 9, 65536], P(None, None, ('grp', 'dom'))
The draws below stay inside these ranges and needn't reach their ends.
Inputs may be any that keep to these rules, and one draw needn't show every extreme that they name: `nbr_slot`: on each device, the values below 128 name a local element whose face nbr_face[f, e] names element e back through face f; the value 128 + s names received slot s, and every slot 0 to 383 is named by exactly one face of the device. For a face that names a received slot whose sending device exists, nbr_face is the face c // 128 of the sender's send_slot entry c for that slot; where the sender does not exist it is arbitrary. `send_slot`: on each device, 384 distinct values f * 128 + e naming faces of its own elements; none of these faces has a local neighbour.
All inputs are finite; a program needn't handle non-finite values.
Results may differ from the reference program's by a relative error of at most 0.0003.
Values sent between devices are 32-bit elements; how exact they have to be, the bound alone decides.
No kernel may reach another device: no remote copies, remote signals or barrier semaphores. Data moves between devices by JAX's collectives and lax.ppermute only.
A program may use at most 64 MiB of HBM per device.

```python
import math
import jax
import jax.numpy as jnp
from jax import lax

ORDER = 6
NQ = 9
NB = 56
NF = 21
ELEM_DEV = 128
HALO_DOM = 128
HALO_GRP = 64
SENDS = 384
ELEMS = 65536
N_GRP = 8
N_DOM = 64


def topology(key):
    elem_count = ELEM_DEV
    halo_dom = elem_count
    halo_grp = elem_count // 2
    sends_count = 2 * halo_dom + 2 * halo_grp
    face_count = 4 * elem_count
    devices_all = N_GRP * N_DOM
    keys_all = jax.random.split(jax.random.fold_in(key, 7), devices_all)
    permuted = jax.vmap(lambda one_key: jax.random.permutation(one_key, face_count))(keys_all)
    permuted = permuted.astype(jnp.int32).reshape(N_GRP, N_DOM, face_count)
    lower_dom = jnp.roll(permuted, 1, axis=1)[:, :, halo_dom:2 * halo_dom]
    upper_dom = jnp.roll(permuted, -1, axis=1)[:, :, 0:halo_dom]
    lower_grp = jnp.roll(permuted, 1, axis=0)[:, :, 2 * halo_dom + halo_grp:sends_count]
    upper_grp = jnp.roll(permuted, -1, axis=0)[:, :, 2 * halo_dom:2 * halo_dom + halo_grp]
    peer_faces = jnp.concatenate([lower_dom, upper_dom, lower_grp, upper_grp], axis=2)
    local_faces = permuted[:, :, sends_count:]
    pairing = jnp.arange(face_count - sends_count, dtype=jnp.int32) ^ 1
    partner = local_faces[:, :, pairing]
    halo_values = jnp.broadcast_to(elem_count + jnp.arange(sends_count, dtype=jnp.int32), peer_faces.shape)
    slot_values = jnp.concatenate([halo_values, partner % elem_count], axis=2)
    face_values = jnp.concatenate([peer_faces // elem_count, partner // elem_count], axis=2)

    def place_values(positions, values):
        return jnp.zeros((face_count,), jnp.int32).at[positions].set(values)
    flat_perms = permuted.reshape(devices_all, face_count)
    slot_table = jax.vmap(place_values)(flat_perms, slot_values.reshape(devices_all, face_count))
    face_ids = jax.vmap(place_values)(flat_perms, face_values.reshape(devices_all, face_count))

    def arrange(per_device):
        return jnp.transpose(per_device.reshape(devices_all, 4, elem_count), (1, 0, 2)).reshape(4, devices_all * elem_count)
    return (arrange(slot_table), arrange(face_ids), permuted[:, :, :sends_count].reshape(-1))


def draw_nbr_slot(key, part):
    return topology(key)[0]


def draw_nbr_face(key, part):
    return topology(key)[1]


def draw_send_slot(key, part):
    return topology(key)[2]


def level_of(stream_key, dims, pieces, least, high):
    def one(dim, shards_of):
        heights = jax.random.uniform(jax.random.fold_in(jax.random.fold_in(stream_key, 6), dim), (shards_of,), jnp.float32, least / len(pieces), high / len(pieces))
        return jnp.repeat(jnp.exp(heights), dims[dim] // shards_of).reshape((-1,) + (1,) * (len(dims) - dim - 1))

    level = one(*pieces[0])
    for cut in pieces[1:]:
        level = level * one(*cut)
    return level


def bell_draw(own_key, shape, spread, limit, pieces=(), held_as=jnp.bfloat16):
    factor_of = level_of(own_key, shape, pieces, -0.22, 0.18) if pieces else 1.0
    result = jax.random.normal(own_key, shape, jnp.float32) * spread * factor_of
    return jnp.minimum(jnp.maximum(result, -limit), limit).astype(held_as)


def setup_inputs(seed: int = 0) -> dict:
    keys = jax.random.split(jax.random.key(seed), 11)
    return {
        "state": bell_draw(keys[0], (NB, NQ, ELEMS), 1.0, 6.0, ((2, 512),), jnp.float32),
        "star": bell_draw(keys[1], (3, NQ, NQ, ELEMS), 0.3, 1.75, ((3, 512),), jnp.float32),
        "flux_own": bell_draw(keys[2], (4, NQ, NQ, ELEMS), 0.15, 0.875, ((3, 512),), jnp.float32),
        "flux_nbr": bell_draw(keys[3], (4, NQ, NQ, ELEMS), 0.15, 0.875, ((3, 512),), jnp.float32),
        "stiff": bell_draw(keys[4], (3, NB, NB), NB ** -0.5, 0.75, (), jnp.float32),
        "trace": bell_draw(keys[5], (4, NF, NB), NB ** -0.5, 0.75, (), jnp.float32),
        "lift": bell_draw(keys[6], (4, NB, NF), NF ** -0.5, 1.25, (), jnp.float32),
        "nbr_slot": draw_nbr_slot(jax.random.fold_in(keys[10], 71), 0),
        "nbr_face": draw_nbr_face(jax.random.fold_in(keys[10], 71), 0),
        "send_slot": draw_send_slot(jax.random.fold_in(keys[10], 71), 0),
    }


exact_prec = lax.Precision.HIGHEST


def mix_quantities(block_data, matrices):
    return jnp.einsum("lpe,pqe->lqe", block_data, matrices, precision=exact_prec)


def apply_basis(matrix, field_data):
    elem_count = field_data.shape[2]
    product = jnp.dot(matrix, field_data.reshape(field_data.shape[0], -1), precision=exact_prec)
    return product.reshape(matrix.shape[0], field_data.shape[1], elem_count)


def taylor_terms(state_now, star, stiff):
    taylor_list = [state_now]
    for order_k in range(ORDER - 1):
        previous = taylor_list[-1]
        summed = mix_quantities(apply_basis(stiff[0], previous), star[0])
        for axis_d in range(1, 3):
            summed = summed + mix_quantities(apply_basis(stiff[axis_d], previous), star[axis_d])
        taylor_list.append(-summed)
    return taylor_list


def integrate(taylor_list, start_time, stop_time):
    summed = jnp.zeros_like(taylor_list[0])
    for order_k, term_now in enumerate(taylor_list):
        weight = (stop_time ** (order_k + 1) - start_time ** (order_k + 1)) / math.factorial(order_k + 1)
        summed = summed + weight * term_now
    return summed


def face_table(integral, trace):
    elem_count = integral.shape[2]
    per_face = [apply_basis(trace[face_f], integral) for face_f in range(4)]
    return jnp.concatenate(per_face, axis=2).reshape(-1, 4 * elem_count)


def update(base_state, integral, own_table, nbr_table, star, flux_own, flux_nbr, stiff, lift):
    elem_count = integral.shape[2]
    face_basis = lift.shape[2]
    quantities = integral.shape[1]
    summed = mix_quantities(apply_basis(stiff[0].T, integral), star[0])
    for axis_d in range(1, 3):
        summed = summed + mix_quantities(apply_basis(stiff[axis_d].T, integral), star[axis_d])
    blocks = []
    for face_f in range(4):
        own_part = own_table[:, face_f * elem_count:(face_f + 1) * elem_count].reshape(face_basis, quantities, elem_count)
        other_part = nbr_table[:, face_f * elem_count:(face_f + 1) * elem_count].reshape(face_basis, quantities, elem_count)
        blocks.append(mix_quantities(own_part, flux_own[face_f]) + mix_quantities(other_part, flux_nbr[face_f]))
    stacked = jnp.concatenate(blocks, axis=0)
    lift_flat = jnp.transpose(lift, (1, 0, 2)).reshape(lift.shape[1], -1)
    flux_total = apply_basis(lift_flat, stacked)
    return base_state + summed - flux_total


def gather_faces(local_part, received, slots, face_ids):
    elem_count = slots.shape[1]
    combined = jnp.concatenate([local_part, received], axis=1)
    columns = jnp.where(slots < elem_count, face_ids * elem_count + slots, slots + 3 * elem_count)
    return jnp.take(combined, columns.reshape(-1), axis=1)


def receive(sent):
    shaped = sent.reshape(N_GRP, N_DOM, sent.shape[1], sent.shape[2])
    to_lower = shaped[..., :HALO_DOM]
    to_upper = shaped[..., HALO_DOM:2 * HALO_DOM]
    grp_lower = shaped[..., 2 * HALO_DOM:2 * HALO_DOM + HALO_GRP]
    grp_upper = shaped[..., 2 * HALO_DOM + HALO_GRP:]
    zero_dom = jnp.zeros_like(to_lower[:, :1])
    zero_grp = jnp.zeros_like(grp_lower[:1])
    from_lower = jnp.concatenate([zero_dom, to_upper[:, :-1]], axis=1)
    from_upper = jnp.concatenate([to_lower[:, 1:], zero_dom], axis=1)
    from_glower = jnp.concatenate([zero_grp, grp_upper[:-1]], axis=0)
    from_gupper = jnp.concatenate([grp_lower[1:], zero_grp], axis=0)
    joined = jnp.concatenate([from_lower, from_upper, from_glower, from_gupper], axis=3)
    return joined.reshape(sent.shape)


def reference(state, star, flux_own, flux_nbr, stiff, trace, lift, nbr_slot, nbr_face, send_slot):
    elem_count = ELEM_DEV
    devices_all = N_GRP * N_DOM

    def device_slice(source, index_dev):
        return lax.dynamic_slice_in_dim(source, index_dev * elem_count, elem_count, axis=source.ndim - 1)

    def sends_of(index_dev):
        return lax.dynamic_slice_in_dim(send_slot, index_dev * SENDS, SENDS, axis=0)

    def first_pass(index_dev):
        is_fault = index_dev < N_DOM
        taylor_list = taylor_terms(device_slice(state, index_dev), device_slice(star, index_dev), stiff)
        first_half = integrate(taylor_list, 0.0, 0.5)
        later_half = integrate(taylor_list, 0.5, 1.0)
        table_one = face_table(first_half, trace)
        table_later = face_table(later_half, trace)
        chosen = sends_of(index_dev)
        main_integ = jnp.where(is_fault, first_half, first_half + later_half)
        main_table = jnp.where(is_fault, table_one, table_one + table_later)
        return main_integ, main_table, jnp.take(table_one, chosen, axis=1), jnp.take(table_later, chosen, axis=1)

    main_integ, main_table, sent_one, sent_later = lax.map(first_pass, jnp.arange(devices_all, dtype=jnp.int32))
    recv_one = receive(sent_one)

    def fault_pass(index_dev):
        star_here = device_slice(star, index_dev)
        nbr_one = gather_faces(main_table[index_dev], recv_one[index_dev], device_slice(nbr_slot, index_dev), device_slice(nbr_face, index_dev))
        mid_state = update(device_slice(state, index_dev), main_integ[index_dev], main_table[index_dev], nbr_one, star_here, device_slice(flux_own, index_dev), device_slice(flux_nbr, index_dev), stiff, lift)
        second_half = integrate(taylor_terms(mid_state, star_here, stiff), 0.0, 0.5)
        table_two = face_table(second_half, trace)
        return mid_state, second_half, table_two, jnp.take(table_two, sends_of(index_dev), axis=1)

    mid_states, seconds, tables_two, sent_fault = lax.map(fault_pass, jnp.arange(N_DOM, dtype=jnp.int32))
    recv_two = receive(sent_later.at[:N_DOM].set(sent_fault))

    def final_pass(index_dev):
        is_fault = index_dev < N_DOM
        fault_index = jnp.minimum(index_dev, N_DOM - 1)
        base_state = jnp.where(is_fault, mid_states[fault_index], device_slice(state, index_dev))
        integral = jnp.where(is_fault, seconds[fault_index], main_integ[index_dev])
        local_part = jnp.where(is_fault, tables_two[fault_index], main_table[index_dev])
        received = recv_two[index_dev] + jnp.where(is_fault, 0.0, recv_one[index_dev])
        nbr_table = gather_faces(local_part, received, device_slice(nbr_slot, index_dev), device_slice(nbr_face, index_dev))
        return update(base_state, integral, local_part, nbr_table, device_slice(star, index_dev), device_slice(flux_own, index_dev), device_slice(flux_nbr, index_dev), stiff, lift)

    outputs = lax.map(final_pass, jnp.arange(devices_all, dtype=jnp.int32))
    return jnp.moveaxis(outputs, 0, 2).reshape(NB, NQ, -1)
```

```python
import math

import jax
import jax.numpy as jnp
from jax import lax
from jax.experimental import pallas as pl
from jax.experimental.pallas import tpu as pltpu
from jax.sharding import PartitionSpec as P

ORDER = 6
NB = 56
NQ = 9
NF = 21
FP = 24
E = 128
LN = NQ * E
TR = NQ * FP
KP = 256

HI = lax.Precision.HIGHEST
F32 = jnp.float32

W_FIRST = [0.5 ** (k + 1) / math.factorial(k + 1) for k in range(ORDER)]
W_LATER = [(1.0 - 0.5 ** (k + 1)) / math.factorial(k + 1) for k in range(ORDER)]


def _dot(a, b):
    return jnp.dot(a, b, precision=HI, preferred_element_type=F32)


def _mix_vol(x_ref, star_ref, y_ref):
    for d in range(3):
        for q in range(NQ):
            acc = None
            for p in range(NQ):
                t = x_ref[:, p * E:(p + 1) * E] * star_ref[d, p, q:q + 1, :]
                acc = t if acc is None else acc + t
            y_ref[d * NB:(d + 1) * NB, q * E:(q + 1) * E] = acc


def _taylor(x_ref, star_ref, stiffc, d_ref, y_ref, accs):
    x = x_ref[...]
    for ref, w in accs:
        ref[...] = w[0] * x
    d_ref[...] = x
    for k in range(ORDER - 1):
        _mix_vol(d_ref, star_ref, y_ref)
        dn = -_dot(stiffc, y_ref[...])
        d_ref[...] = dn
        for ref, w in accs:
            ref[...] = ref[...] + w[k + 1] * dn


def _table(x_ref, trace_ref, yt_ref, t_ref):
    yt_ref[...] = _dot(trace_ref[...], x_ref[...])
    for f in range(4):
        for p in range(NQ):
            t_ref[p * FP:(p + 1) * FP, f * E:(f + 1) * E] = yt_ref[f * FP:(f + 1) * FP, p * E:(p + 1) * E]


def _send(t_ref, send_ref, lo_ref, hi_ref, g_ref):
    rows = lax.broadcasted_iota(jnp.int32, (4 * E, 3 * E), 0)
    onehot = jnp.where(rows == send_ref[...], 1.0, 0.0).astype(F32)
    s = _dot(t_ref[...], onehot)
    lo_ref[...] = s[:, 0:E]
    hi_ref[...] = s[:, E:2 * E]
    g_ref[...] = s[:, 2 * E:3 * E]


def _gather(comb, slot_ref, face_ref, g_ref):
    rows = lax.broadcasted_iota(jnp.int32, (8 * E, E), 0)
    for f in range(4):
        v = slot_ref[f:f + 1, :]
        nf = face_ref[f:f + 1, :]
        s = v - E
        src = jnp.where(v < E, nf * E + v, 4 * E + s + jnp.where(s >= 2 * E, 64, 0))
        onehot = jnp.where(rows == src, 1.0, 0.0).astype(F32)
        g_ref[:, f * E:(f + 1) * E] = _dot(comb, onehot)


def _update(b_ref, x_ref, s_ref, g_ref, star_ref, fo_ref, fn_ref, stiffT, lift, y_ref, yf_ref, out_ref):
    _mix_vol(x_ref, star_ref, y_ref)
    vol = _dot(stiffT, y_ref[...])
    for f in range(4):
        for q in range(NQ):
            acc = None
            for p in range(NQ):
                t = (s_ref[p * FP:(p + 1) * FP, f * E:(f + 1) * E] * fo_ref[f, p, q:q + 1, :]
                     + g_ref[p * FP:(p + 1) * FP, f * E:(f + 1) * E] * fn_ref[f, p, q:q + 1, :])
                acc = t if acc is None else acc + t
            yf_ref[f * FP:(f + 1) * FP, q * E:(q + 1) * E] = acc
    ftot = _dot(lift, yf_ref[...])
    out_ref[...] = (b_ref[...] + vol) - ftot


def _kernel_a(x_ref, star_ref, consts_ref, trace_ref, send_ref,
              first_ref, fl_ref, t1_ref, t1l_ref, s1lo, s1hi, s1g, sllo, slhi, slg,
              d_ref, y_ref, yt_ref, later_ref, tl_ref):
    y_ref[3 * NB:KP, :] = jnp.zeros((KP - 3 * NB, LN), F32)
    stiffc = consts_ref[:, 0:KP]
    _taylor(x_ref, star_ref, stiffc, d_ref, y_ref, [(first_ref, W_FIRST), (later_ref, W_LATER)])
    fl_ref[...] = first_ref[...] + later_ref[...]
    _table(first_ref, trace_ref, yt_ref, t1_ref)
    _table(later_ref, trace_ref, yt_ref, tl_ref)
    t1l_ref[...] = t1_ref[...] + tl_ref[...]
    _send(t1_ref, send_ref, s1lo, s1hi, s1g)
    _send(tl_ref, send_ref, sllo, slhi, slg)


def _kernel_b(flag_ref, x_ref, first_ref, fl_ref, t1_ref, t1l_ref, sllo, slhi, slg,
              r1lo, r1hi, r1glo, r1ghi, slot_ref, face_ref, star_ref, fo_ref, fn_ref,
              consts_ref, trace_ref, send_ref,
              base_ref, integ_ref, own_ref, s2lo, s2hi, s2g,
              d_ref, y_ref, yt_ref, yf_ref, g_ref):
    fault = flag_ref[0] == 1

    @pl.when(fault)
    def _():
        y_ref[3 * NB:KP, :] = jnp.zeros((KP - 3 * NB, LN), F32)
        comb = jnp.concatenate([t1_ref[...], r1lo[...], r1hi[...], r1glo[...], r1ghi[...]], axis=1)
        _gather(comb, slot_ref, face_ref, g_ref)
        _update(x_ref, first_ref, t1_ref, g_ref, star_ref, fo_ref, fn_ref,
                consts_ref[:, KP:2 * KP], consts_ref[:, 2 * KP:2 * KP + 4 * FP], y_ref, yf_ref, base_ref)
        _taylor(base_ref, star_ref, consts_ref[:, 0:KP], d_ref, y_ref, [(integ_ref, W_FIRST)])
        _table(integ_ref, trace_ref, yt_ref, own_ref)
        _send(own_ref, send_ref, s2lo, s2hi, s2g)

    @pl.when(jnp.logical_not(fault))
    def _():
        base_ref[...] = x_ref[...]
        integ_ref[...] = fl_ref[...]
        own_ref[...] = t1l_ref[...]
        s2lo[...] = sllo[...]
        s2hi[...] = slhi[...]
        s2g[...] = slg[...]


def _kernel_c(flag_ref, base_ref, integ_ref, own_ref, r1lo, r1hi, r1glo, r1ghi,
              r2lo, r2hi, r2glo, r2ghi, slot_ref, face_ref, star_ref, fo_ref, fn_ref, consts_ref,
              out_ref, y_ref, yf_ref, g_ref):
    keep = (1 - flag_ref[0]).astype(F32)
    y_ref[3 * NB:KP, :] = jnp.zeros((KP - 3 * NB, LN), F32)
    comb = jnp.concatenate(
        [own_ref[...], r2lo[...] + keep * r1lo[...], r2hi[...] + keep * r1hi[...],
         r2glo[...] + keep * r1glo[...], r2ghi[...] + keep * r1ghi[...]], axis=1)
    _gather(comb, slot_ref, face_ref, g_ref)
    _update(base_ref, integ_ref, own_ref, g_ref, star_ref, fo_ref, fn_ref,
            consts_ref[:, KP:2 * KP], consts_ref[:, 2 * KP:2 * KP + 4 * FP], y_ref, yf_ref, out_ref)


def _vmem():
    return pl.BlockSpec(memory_space=pltpu.VMEM)


def _smem():
    return pl.BlockSpec(memory_space=pltpu.SMEM)


def _sds(shape):
    return jax.ShapeDtypeStruct(shape, F32)


def exchange(lo, hi, g):
    n_dom = lax.axis_size("dom")
    n_grp = lax.axis_size("grp")
    from_lo = lax.ppermute(hi, "dom", [(i, i + 1) for i in range(n_dom - 1)])
    from_hi = lax.ppermute(lo, "dom", [(i + 1, i) for i in range(n_dom - 1)])
    from_glo = lax.ppermute(g, "grp", [(i, i + 1) for i in range(n_grp - 1)])
    from_ghi = lax.ppermute(g, "grp", [(i + 1, i) for i in range(n_grp - 1)])
    return from_lo, from_hi, from_glo, from_ghi


def local(state, star, flux_own, flux_nbr, stiff, trace, lift, nbr_slot, nbr_face, send_slot):
    flag = (lax.axis_index("grp") == 0).astype(jnp.int32).reshape(1)
    x0 = state.reshape(NB, LN)
    stiff_cat = jnp.concatenate([stiff[0], stiff[1], stiff[2]], axis=1)
    stiff_t_cat = jnp.concatenate([stiff[0].T, stiff[1].T, stiff[2].T], axis=1)
    lift_cat = jnp.transpose(jnp.pad(lift, ((0, 0), (0, 0), (0, FP - NF))), (1, 0, 2)).reshape(NB, 4 * FP)
    consts = jnp.concatenate(
        [jnp.pad(stiff_cat, ((0, 0), (0, KP - 3 * NB))),
         jnp.pad(stiff_t_cat, ((0, 0), (0, KP - 3 * NB))),
         jnp.pad(lift_cat, ((0, 0), (0, 128 - 4 * FP)))], axis=1)
    trace_pad = jnp.pad(trace, ((0, 0), (0, FP - NF), (0, 0))).reshape(4 * FP, NB)
    send = send_slot.reshape(1, 3 * E)

    field = _sds((NB, LN))
    table = _sds((TR, 4 * E))
    part = _sds((TR, E))
    outs_a = pl.pallas_call(
        _kernel_a,
        out_shape=(field, field, table, table, part, part, part, part, part, part),
        in_specs=[_vmem()] * 5,
        out_specs=tuple([_vmem()] * 10),
        scratch_shapes=[pltpu.VMEM((NB, LN), F32), pltpu.VMEM((KP, LN), F32), pltpu.VMEM((4 * FP, LN), F32),
                        pltpu.VMEM((NB, LN), F32), pltpu.VMEM((TR, 4 * E), F32)],
    )(x0, star, consts, trace_pad, send)
    first, fl, t1, t1l, s1lo, s1hi, s1g, sllo, slhi, slg = outs_a

    r1 = exchange(s1lo, s1hi, s1g)

    outs_b = pl.pallas_call(
        _kernel_b,
        out_shape=(field, field, table, part, part, part),
        in_specs=[_smem()] + [_vmem()] * 20,
        out_specs=tuple([_vmem()] * 6),
        scratch_shapes=[pltpu.VMEM((NB, LN), F32), pltpu.VMEM((KP, LN), F32), pltpu.VMEM((4 * FP, LN), F32),
                        pltpu.VMEM((4 * FP, LN), F32), pltpu.VMEM((TR, 4 * E), F32)],
    )(flag, x0, first, fl, t1, t1l, sllo, slhi, slg, *r1, nbr_slot, nbr_face, star, flux_own, flux_nbr,
      consts, trace_pad, send)
    base, integ, own, s2lo, s2hi, s2g = outs_b

    r2 = exchange(s2lo, s2hi, s2g)

    out = pl.pallas_call(
        _kernel_c,
        out_shape=field,
        in_specs=[_smem()] + [_vmem()] * 17,
        out_specs=_vmem(),
        scratch_shapes=[pltpu.VMEM((KP, LN), F32), pltpu.VMEM((4 * FP, LN), F32), pltpu.VMEM((TR, 4 * E), F32)],
    )(flag, base, integ, own, *r1, *r2, nbr_slot, nbr_face, star, flux_own, flux_nbr, consts)
    return out.reshape(NB, NQ, E)


def solution(mesh):
    in_specs = (
        P(None, None, ("grp", "dom")),
        P(None, None, None, ("grp", "dom")),
        P(None, None, None, ("grp", "dom")),
        P(None, None, None, ("grp", "dom")),
        P(),
        P(),
        P(),
        P(None, ("grp", "dom")),
        P(None, ("grp", "dom")),
        P(("grp", "dom")),
    )
    out_specs = P(None, None, ("grp", "dom"))
    return jax.shard_map(local, mesh=mesh, in_specs=in_specs, out_specs=out_specs, check_vma=False)
```

```python
import math

import jax
import jax.numpy as jnp
from jax import lax
from jax.experimental import pallas as pl
from jax.experimental.pallas import tpu as pltpu
from jax.sharding import PartitionSpec as P

ORDER = 6
NB = 56
NQ = 9
NF = 21
FP = 24
E = 128
LN = NQ * E
TR = NQ * FP

F32 = jnp.float32

W_FIRST = [0.5 ** (k + 1) / math.factorial(k + 1) for k in range(ORDER)]
W_LATER = [(1.0 - 0.5 ** (k + 1)) / math.factorial(k + 1) for k in range(ORDER)]


BF = jnp.bfloat16


def _bdot(a, b):
    return jnp.dot(a, b, preferred_element_type=F32)


def _split2(x):
    hi = x.astype(BF)
    return hi, (x - hi.astype(F32)).astype(BF)


def _dot3(a, b):
    return _bdot(a[0], b[0]) + (_bdot(a[0], b[1]) + _bdot(a[1], b[0]))


def _split3(x):
    hi = x.astype(BF)
    r = x - hi.astype(F32)
    mid = r.astype(BF)
    return hi, mid, (r - mid.astype(F32)).astype(BF)


def _sel(parts, onehot):
    return (_bdot(parts[0], onehot) + _bdot(parts[1], onehot)) + _bdot(parts[2], onehot)


def _load_field(ref):
    return jnp.concatenate([ref[p] for p in range(NQ)], axis=1)


def _store_field(ref, val):
    for q in range(NQ):
        ref[q] = val[:, q * E:(q + 1) * E]


def _mix_vol(a_ref, star_ref, out_ref, sign):
    for q in range(NQ):
        acc = None
        for d in range(3):
            for p in range(NQ):
                t = a_ref[d * NB:(d + 1) * NB, p * E:(p + 1) * E] * star_ref[d, p, q:q + 1, :]
                acc = t if acc is None else acc + t
        out_ref[:, q * E:(q + 1) * E] = acc if sign > 0 else -acc


def _taylor(x, star_ref, stiff_p, d_ref, a_ref, accs):
    for ref, w in accs:
        ref[...] = w[0] * x
    d_ref[...] = x
    for k in range(ORDER - 1):
        a_ref[...] = _dot3(stiff_p, _split2(d_ref[...]))
        _mix_vol(a_ref, star_ref, d_ref, -1)
        dn = d_ref[...]
        for ref, w in accs:
            ref[...] = ref[...] + w[k + 1] * dn


def _table(x, trace_ref, t_ref):
    xp = _split2(x)
    t_ref[...] = jnp.zeros(t_ref.shape, F32)
    for f in range(4):
        yt = _dot3(_split2(trace_ref[f]), xp)
        for p in range(NQ):
            t_ref[p * FP:p * FP + NF, f * E:(f + 1) * E] = yt[:, p * E:(p + 1) * E]


def _send(tables, send_ref, outs):
    rows = lax.broadcasted_iota(jnp.int32, (4 * E, 3 * E), 0)
    onehot = jnp.where(rows == send_ref[...], 1.0, 0.0).astype(BF)
    s = _sel(_split3(jnp.concatenate(tables, axis=0)), onehot)
    for i, (lo_ref, hi_ref, g_ref) in enumerate(outs):
        blk = s[i * TR:(i + 1) * TR]
        lo_ref[...] = blk[:, 0:E]
        hi_ref[...] = blk[:, E:2 * E]
        g_ref[...] = blk[:, 2 * E:3 * E]


def _gather(comb, slot_ref, face_ref, g_ref):
    rows = lax.broadcasted_iota(jnp.int32, (8 * E, E), 0)
    parts = _split3(comb)
    for f in range(4):
        v = slot_ref[f:f + 1, :]
        nf = face_ref[f:f + 1, :]
        s = v - E
        src = jnp.where(v < E, nf * E + v, 4 * E + s + jnp.where(s >= 2 * E, 64, 0))
        onehot = jnp.where(rows == src, 1.0, 0.0).astype(BF)
        g_ref[:, f * E:(f + 1) * E] = _sel(parts, onehot)


def _update(b, x, s_ref, g_ref, star_ref, fo_ref, fn_ref, stiff_t_p, lift_p, a_ref, v_ref, yf_ref):
    a_ref[...] = _dot3(stiff_t_p, _split2(x))
    _mix_vol(a_ref, star_ref, v_ref, 1)
    for f in range(4):
        for q in range(NQ):
            acc = None
            for p in range(NQ):
                t = (s_ref[p * FP:(p + 1) * FP, f * E:(f + 1) * E] * fo_ref[f, p, q:q + 1, :]
                     + g_ref[p * FP:(p + 1) * FP, f * E:(f + 1) * E] * fn_ref[f, p, q:q + 1, :])
                acc = t if acc is None else acc + t
            yf_ref[f * FP:(f + 1) * FP, q * E:(q + 1) * E] = acc
    ftot = _dot3(lift_p, _split2(yf_ref[...]))
    return (b + v_ref[...]) - ftot


def _kernel_a(x_ref, star_ref, stiff_ref, trace_ref, send_ref,
              first_ref, fl_ref, t1_ref, t1l_ref, s1lo, s1hi, s1g, sllo, slhi, slg,
              d_ref, a_ref, acc1_ref, acc2_ref, tl_ref):
    x = _load_field(x_ref)
    _taylor(x, star_ref, _split2(stiff_ref[...]), d_ref, a_ref, [(acc1_ref, W_FIRST), (acc2_ref, W_LATER)])
    first = acc1_ref[...]
    later = acc2_ref[...]
    _store_field(first_ref, first)
    _store_field(fl_ref, first + later)
    _table(first, trace_ref, t1_ref)
    _table(later, trace_ref, tl_ref)
    t1l_ref[...] = t1_ref[...] + tl_ref[...]
    _send([t1_ref[...], tl_ref[...]], send_ref, [(s1lo, s1hi, s1g), (sllo, slhi, slg)])


def _kernel_b(flag_ref, x_ref, first_ref, fl_ref, t1_ref, t1l_ref, sllo, slhi, slg,
              r1lo, r1hi, r1glo, r1ghi, slot_ref, face_ref, star_ref, fo_ref, fn_ref,
              stiff_ref, stiff_t_ref, lift_ref, trace_ref, send_ref,
              base_ref, integ_ref, own_ref, s2lo, s2hi, s2g,
              d_ref, a_ref, v_ref, yf_ref, g_ref, acc_ref):
    fault = flag_ref[0] == 1

    @pl.when(fault)
    def _():
        comb = jnp.concatenate([t1_ref[...], r1lo[...], r1hi[...], r1glo[...], r1ghi[...]], axis=1)
        _gather(comb, slot_ref, face_ref, g_ref)
        mid = _update(_load_field(x_ref), _load_field(first_ref), t1_ref, g_ref, star_ref, fo_ref, fn_ref,
                      _split2(stiff_t_ref[...]), _split2(lift_ref[...]), a_ref, v_ref, yf_ref)
        _store_field(base_ref, mid)
        _taylor(mid, star_ref, _split2(stiff_ref[...]), d_ref, a_ref, [(acc_ref, W_FIRST)])
        second = acc_ref[...]
        _store_field(integ_ref, second)
        _table(second, trace_ref, own_ref)
        _send([own_ref[...]], send_ref, [(s2lo, s2hi, s2g)])

    @pl.when(jnp.logical_not(fault))
    def _():
        base_ref[...] = x_ref[...]
        integ_ref[...] = fl_ref[...]
        own_ref[...] = t1l_ref[...]
        s2lo[...] = sllo[...]
        s2hi[...] = slhi[...]
        s2g[...] = slg[...]


def _kernel_c(flag_ref, base_ref, integ_ref, own_ref, r1lo, r1hi, r1glo, r1ghi,
              r2lo, r2hi, r2glo, r2ghi, slot_ref, face_ref, star_ref, fo_ref, fn_ref,
              stiff_t_ref, lift_ref,
              out_ref, a_ref, v_ref, yf_ref, g_ref):
    keep = (1 - flag_ref[0]).astype(F32)
    comb = jnp.concatenate(
        [own_ref[...], r2lo[...] + keep * r1lo[...], r2hi[...] + keep * r1hi[...],
         r2glo[...] + keep * r1glo[...], r2ghi[...] + keep * r1ghi[...]], axis=1)
    _gather(comb, slot_ref, face_ref, g_ref)
    out = _update(_load_field(base_ref), _load_field(integ_ref), own_ref, g_ref, star_ref, fo_ref, fn_ref,
                  _split2(stiff_t_ref[...]), _split2(lift_ref[...]), a_ref, v_ref, yf_ref)
    _store_field(out_ref, out)


def _vmem():
    return pl.BlockSpec(memory_space=pltpu.VMEM)


def _smem():
    return pl.BlockSpec(memory_space=pltpu.SMEM)


def _sds(shape):
    return jax.ShapeDtypeStruct(shape, F32)


def exchange(lo, hi, g):
    n_dom = lax.axis_size("dom")
    n_grp = lax.axis_size("grp")
    from_lo = lax.ppermute(hi, "dom", [(i, i + 1) for i in range(n_dom - 1)])
    from_hi = lax.ppermute(lo, "dom", [(i + 1, i) for i in range(n_dom - 1)])
    from_glo = lax.ppermute(g, "grp", [(i, i + 1) for i in range(n_grp - 1)])
    from_ghi = lax.ppermute(g, "grp", [(i + 1, i) for i in range(n_grp - 1)])
    return from_lo, from_hi, from_glo, from_ghi


def local(state, star, flux_own, flux_nbr, stiff, trace, lift, nbr_slot, nbr_face, send_slot):
    flag = (lax.axis_index("grp") == 0).astype(jnp.int32).reshape(1)
    x0 = jnp.transpose(state, (1, 0, 2))
    stiff_st = stiff.reshape(3 * NB, NB)
    stiff_t_st = jnp.transpose(stiff, (0, 2, 1)).reshape(3 * NB, NB)
    lift_cat = jnp.transpose(jnp.pad(lift, ((0, 0), (0, 0), (0, FP - NF))), (1, 0, 2)).reshape(NB, 4 * FP)
    send = send_slot.reshape(1, 3 * E)

    field = _sds((NQ, NB, E))
    table = _sds((TR, 4 * E))
    part = _sds((TR, E))
    wide = pltpu.VMEM((NB, LN), F32)
    outs_a = pl.pallas_call(
        _kernel_a,
        out_shape=(field, field, table, table, part, part, part, part, part, part),
        in_specs=[_vmem()] * 5,
        out_specs=tuple([_vmem()] * 10),
        scratch_shapes=[wide, pltpu.VMEM((3 * NB, LN), F32), wide, wide, pltpu.VMEM((TR, 4 * E), F32)],
    )(x0, star, stiff_st, trace, send)
    first, fl, t1, t1l, s1lo, s1hi, s1g, sllo, slhi, slg = outs_a

    r1 = exchange(s1lo, s1hi, s1g)

    outs_b = pl.pallas_call(
        _kernel_b,
        out_shape=(field, field, table, part, part, part),
        in_specs=[_smem()] + [_vmem()] * 22,
        out_specs=tuple([_vmem()] * 6),
        scratch_shapes=[wide, pltpu.VMEM((3 * NB, LN), F32), wide, pltpu.VMEM((4 * FP, LN), F32),
                        pltpu.VMEM((TR, 4 * E), F32), wide],
    )(flag, x0, first, fl, t1, t1l, sllo, slhi, slg, *r1, nbr_slot, nbr_face, star, flux_own, flux_nbr,
      stiff_st, stiff_t_st, lift_cat, trace, send)
    base, integ, own, s2lo, s2hi, s2g = outs_b

    r2 = exchange(s2lo, s2hi, s2g)

    out = pl.pallas_call(
        _kernel_c,
        out_shape=field,
        in_specs=[_smem()] + [_vmem()] * 18,
        out_specs=_vmem(),
        scratch_shapes=[pltpu.VMEM((3 * NB, LN), F32), wide, pltpu.VMEM((4 * FP, LN), F32),
                        pltpu.VMEM((TR, 4 * E), F32)],
    )(flag, base, integ, own, *r1, *r2, nbr_slot, nbr_face, star, flux_own, flux_nbr, stiff_t_st, lift_cat)
    return jnp.transpose(out, (1, 0, 2))


def solution(mesh):
    in_specs = (
        P(None, None, ("grp", "dom")),
        P(None, None, None, ("grp", "dom")),
        P(None, None, None, ("grp", "dom")),
        P(None, None, None, ("grp", "dom")),
        P(),
        P(),
        P(),
        P(None, ("grp", "dom")),
        P(None, ("grp", "dom")),
        P(("grp", "dom")),
    )
    out_specs = P(None, None, ("grp", "dom"))
    return jax.shard_map(local, mesh=mesh, in_specs=in_specs, out_specs=out_specs, check_vma=False)
```

```python
import math

import jax
import jax.numpy as jnp
from jax import lax
from jax.experimental import pallas as pl
from jax.experimental.pallas import tpu as pltpu
from jax.sharding import PartitionSpec as P

ORDER = 6
NB = 56
NQ = 9
NF = 21
FP = 24
E = 128
LN = NQ * E
TR = NQ * FP

F32 = jnp.float32

W_FIRST = [0.5 ** (k + 1) / math.factorial(k + 1) for k in range(ORDER)]
W_LATER = [(1.0 - 0.5 ** (k + 1)) / math.factorial(k + 1) for k in range(ORDER)]


BF = jnp.bfloat16


def _bdot(a, b):
    return jnp.dot(a, b, preferred_element_type=F32)


def _split2(x):
    hi = x.astype(BF)
    return hi, (x - hi.astype(F32)).astype(BF)


def _dot3(a, b):
    return _bdot(a[0], b[0]) + (_bdot(a[0], b[1]) + _bdot(a[1], b[0]))


def _tdot(a, b):
    return lax.dot_general(a, b, (((0,), (0,)), ((), ())), preferred_element_type=F32)


def _dot3_t(a, b):
    return _tdot(a[0], b[0]) + (_tdot(a[0], b[1]) + _tdot(a[1], b[0]))


def _rows84(ref):
    return jnp.concatenate([ref[r] for r in range(NF)], axis=0)


def _split3(x):
    hi = x.astype(BF)
    r = x - hi.astype(F32)
    mid = r.astype(BF)
    return hi, mid, (r - mid.astype(F32)).astype(BF)


def _sel(parts, onehot):
    return (_bdot(parts[0], onehot) + _bdot(parts[1], onehot)) + _bdot(parts[2], onehot)


def _load_field(ref):
    return jnp.concatenate([ref[p] for p in range(NQ)], axis=1)


def _store_field(ref, val):
    for q in range(NQ):
        ref[q] = val[:, q * E:(q + 1) * E]


def _mix_vol(a_ref, star_ref, out_ref, sign):
    for q in range(NQ):
        acc = None
        for p in range(NQ):
            srow = star_ref[p, q]
            for d in range(3):
                t = a_ref[d * NB:(d + 1) * NB, p * E:(p + 1) * E] * srow[d:d + 1, :]
                acc = t if acc is None else acc + t
        out_ref[:, q * E:(q + 1) * E] = acc if sign > 0 else -acc


def _taylor(x, star_ref, stiff_p, d_ref, a_ref, accs):
    for ref, w in accs:
        ref[...] = w[0] * x
    d_ref[...] = x
    for k in range(ORDER - 1):
        a_ref[...] = _dot3(stiff_p, _split2(d_ref[...]))
        _mix_vol(a_ref, star_ref, d_ref, -1)
        dn = d_ref[...]
        for ref, w in accs:
            ref[...] = ref[...] + w[k + 1] * dn


def _table(x, trace_p, yt_ref, t_ref):
    yt = _dot3(trace_p, _split2(x))
    for p in range(NQ):
        yt_ref[p] = yt[:, p * E:(p + 1) * E]
    t_ref[...] = jnp.zeros(t_ref.shape, F32)
    for f in range(4):
        for p in range(NQ):
            t_ref[p * FP:p * FP + NF, f * E:(f + 1) * E] = yt_ref[p, pl.ds(f, NF, stride=4), :]


def _send(tables, send_ref, outs):
    rows = lax.broadcasted_iota(jnp.int32, (4 * E, 3 * E), 0)
    onehot = jnp.where(rows == send_ref[...], 1.0, 0.0).astype(BF)
    s = _sel(_split3(jnp.concatenate(tables, axis=0)), onehot)
    for i, (lo_ref, hi_ref, g_ref) in enumerate(outs):
        blk = s[i * TR:(i + 1) * TR]
        lo_ref[...] = blk[:, 0:E]
        hi_ref[...] = blk[:, E:2 * E]
        g_ref[...] = blk[:, 2 * E:3 * E]


def _gather(comb, slot_ref, face_ref, g_ref):
    rows = lax.broadcasted_iota(jnp.int32, (8 * E, E), 0)
    parts = _split3(comb)
    for f in range(4):
        v = slot_ref[f:f + 1, :]
        nf = face_ref[f:f + 1, :]
        s = v - E
        src = jnp.where(v < E, nf * E + v, 4 * E + s + jnp.where(s >= 2 * E, 64, 0))
        onehot = jnp.where(rows == src, 1.0, 0.0).astype(BF)
        g_ref[:, f * E:(f + 1) * E] = _sel(parts, onehot)


def _lift_parts(lift_ref, lt_ref):
    lt_ref[:, 0:NB] = _rows84(lift_ref)
    return [_split2(lt_ref[pl.ds(f, NF, stride=4), 0:NB]) for f in range(4)]


def _update(b, x, s_ref, g_ref, star_ref, fo_ref, fn_ref, stiff_ref, lift_p, a_ref, v_ref, yf_ref):
    xp = _split2(x)
    for d in range(3):
        a_ref[d * NB:(d + 1) * NB, :] = _dot3_t(_split2(stiff_ref[d]), xp)
    _mix_vol(a_ref, star_ref, v_ref, 1)
    for q in range(NQ):
        accs = [None] * 4
        for p in range(NQ):
            orow = fo_ref[p, q]
            nrow = fn_ref[p, q]
            for f in range(4):
                t = (s_ref[p * FP:(p + 1) * FP, f * E:(f + 1) * E] * orow[f:f + 1, :]
                     + g_ref[p * FP:(p + 1) * FP, f * E:(f + 1) * E] * nrow[f:f + 1, :])
                accs[f] = t if accs[f] is None else accs[f] + t
        for f in range(4):
            yf_ref[f * FP:(f + 1) * FP, q * E:(q + 1) * E] = accs[f]
    ftot = None
    for f in range(4):
        t = _dot3_t(lift_p[f], _split2(yf_ref[f * FP:f * FP + NF, :]))
        ftot = t if ftot is None else ftot + t
    return (b + v_ref[...]) - ftot


def _kernel_a(x_ref, star_ref, stiff_ref, trace_ref, send_ref,
              first_ref, fl_ref, t1_ref, t1l_ref, s1lo, s1hi, s1g, sllo, slhi, slg,
              d_ref, a_ref, acc1_ref, acc2_ref, tl_ref, yt_ref):
    x = _load_field(x_ref)
    stiff_st = jnp.concatenate([stiff_ref[d] for d in range(3)], axis=0)
    _taylor(x, star_ref, _split2(stiff_st), d_ref, a_ref, [(acc1_ref, W_FIRST), (acc2_ref, W_LATER)])
    first = acc1_ref[...]
    later = acc2_ref[...]
    _store_field(first_ref, first)
    _store_field(fl_ref, first + later)
    trace_p = _split2(_rows84(trace_ref))
    _table(first, trace_p, yt_ref, t1_ref)
    _table(later, trace_p, yt_ref, tl_ref)
    t1l_ref[...] = t1_ref[...] + tl_ref[...]
    _send([t1_ref[...], tl_ref[...]], send_ref, [(s1lo, s1hi, s1g), (sllo, slhi, slg)])


def _kernel_b(flag_ref, x_ref, first_ref, fl_ref, t1_ref, t1l_ref, sllo, slhi, slg,
              r1lo, r1hi, r1glo, r1ghi, slot_ref, face_ref, star_ref, fo_ref, fn_ref,
              stiff_ref, lift_ref, trace_ref, send_ref,
              base_ref, integ_ref, own_ref, s2lo, s2hi, s2g,
              d_ref, a_ref, v_ref, yf_ref, g_ref, acc_ref, yt_ref, lt_ref):
    fault = flag_ref[0] == 1

    @pl.when(fault)
    def _():
        comb = jnp.concatenate([t1_ref[...], r1lo[...], r1hi[...], r1glo[...], r1ghi[...]], axis=1)
        _gather(comb, slot_ref, face_ref, g_ref)
        mid = _update(_load_field(x_ref), _load_field(first_ref), t1_ref, g_ref, star_ref, fo_ref, fn_ref,
                      stiff_ref, _lift_parts(lift_ref, lt_ref), a_ref, v_ref, yf_ref)
        _store_field(base_ref, mid)
        stiff_st = jnp.concatenate([stiff_ref[d] for d in range(3)], axis=0)
        _taylor(mid, star_ref, _split2(stiff_st), d_ref, a_ref, [(acc_ref, W_FIRST)])
        second = acc_ref[...]
        _store_field(integ_ref, second)
        _table(second, _split2(_rows84(trace_ref)), yt_ref, own_ref)
        _send([own_ref[...]], send_ref, [(s2lo, s2hi, s2g)])

    @pl.when(jnp.logical_not(fault))
    def _():
        base_ref[...] = x_ref[...]
        integ_ref[...] = fl_ref[...]
        own_ref[...] = t1l_ref[...]
        s2lo[...] = sllo[...]
        s2hi[...] = slhi[...]
        s2g[...] = slg[...]


def _kernel_c(flag_ref, base_ref, integ_ref, own_ref, r1lo, r1hi, r1glo, r1ghi,
              r2lo, r2hi, r2glo, r2ghi, slot_ref, face_ref, star_ref, fo_ref, fn_ref,
              stiff_ref, lift_ref,
              out_ref, a_ref, v_ref, yf_ref, g_ref, lt_ref):
    keep = (1 - flag_ref[0]).astype(F32)
    comb = jnp.concatenate(
        [own_ref[...], r2lo[...] + keep * r1lo[...], r2hi[...] + keep * r1hi[...],
         r2glo[...] + keep * r1glo[...], r2ghi[...] + keep * r1ghi[...]], axis=1)
    _gather(comb, slot_ref, face_ref, g_ref)
    out = _update(_load_field(base_ref), _load_field(integ_ref), own_ref, g_ref, star_ref, fo_ref, fn_ref,
                  stiff_ref, _lift_parts(lift_ref, lt_ref), a_ref, v_ref, yf_ref)
    _store_field(out_ref, out)


def _vmem():
    return pl.BlockSpec(memory_space=pltpu.VMEM)


def _smem():
    return pl.BlockSpec(memory_space=pltpu.SMEM)


def _sds(shape):
    return jax.ShapeDtypeStruct(shape, F32)


def exchange(lo, hi, g):
    n_dom = lax.axis_size("dom")
    n_grp = lax.axis_size("grp")
    from_lo = lax.ppermute(hi, "dom", [(i, i + 1) for i in range(n_dom - 1)])
    from_hi = lax.ppermute(lo, "dom", [(i + 1, i) for i in range(n_dom - 1)])
    from_glo = lax.ppermute(g, "grp", [(i, i + 1) for i in range(n_grp - 1)])
    from_ghi = lax.ppermute(g, "grp", [(i + 1, i) for i in range(n_grp - 1)])
    return from_lo, from_hi, from_glo, from_ghi


def local(state, star, flux_own, flux_nbr, stiff, trace, lift, nbr_slot, nbr_face, send_slot):
    flag = (lax.axis_index("grp") == 0).astype(jnp.int32).reshape(1)
    x0 = jnp.transpose(state, (1, 0, 2))
    star = jnp.transpose(star, (1, 2, 0, 3))
    flux_own = jnp.transpose(flux_own, (1, 2, 0, 3))
    flux_nbr = jnp.transpose(flux_nbr, (1, 2, 0, 3))
    trace = jnp.transpose(trace, (1, 0, 2))
    lift = jnp.transpose(lift, (2, 0, 1))
    send = send_slot.reshape(1, 3 * E)

    field = _sds((NQ, NB, E))
    table = _sds((TR, 4 * E))
    part = _sds((TR, E))
    wide = pltpu.VMEM((NB, LN), F32)
    outs_a = pl.pallas_call(
        _kernel_a,
        out_shape=(field, field, table, table, part, part, part, part, part, part),
        in_specs=[_vmem()] * 5,
        out_specs=tuple([_vmem()] * 10),
        scratch_shapes=[wide, pltpu.VMEM((3 * NB, LN), F32), wide, wide, pltpu.VMEM((TR, 4 * E), F32),
                        pltpu.VMEM((NQ, 4 * NF, E), F32)],
    )(x0, star, stiff, trace, send)
    first, fl, t1, t1l, s1lo, s1hi, s1g, sllo, slhi, slg = outs_a

    r1 = exchange(s1lo, s1hi, s1g)

    outs_b = pl.pallas_call(
        _kernel_b,
        out_shape=(field, field, table, part, part, part),
        in_specs=[_smem()] + [_vmem()] * 21,
        out_specs=tuple([_vmem()] * 6),
        scratch_shapes=[wide, pltpu.VMEM((3 * NB, LN), F32), wide, pltpu.VMEM((4 * FP, LN), F32),
                        pltpu.VMEM((TR, 4 * E), F32), wide, pltpu.VMEM((NQ, 4 * NF, E), F32),
                        pltpu.VMEM((4 * NF, E), F32)],
    )(flag, x0, first, fl, t1, t1l, sllo, slhi, slg, *r1, nbr_slot, nbr_face, star, flux_own, flux_nbr,
      stiff, lift, trace, send)
    base, integ, own, s2lo, s2hi, s2g = outs_b

    r2 = exchange(s2lo, s2hi, s2g)

    out = pl.pallas_call(
        _kernel_c,
        out_shape=field,
        in_specs=[_smem()] + [_vmem()] * 18,
        out_specs=_vmem(),
        scratch_shapes=[pltpu.VMEM((3 * NB, LN), F32), wide, pltpu.VMEM((4 * FP, LN), F32),
                        pltpu.VMEM((TR, 4 * E), F32), pltpu.VMEM((4 * NF, E), F32)],
    )(flag, base, integ, own, *r1, *r2, nbr_slot, nbr_face, star, flux_own, flux_nbr, stiff, lift)
    return jnp.transpose(out, (1, 0, 2))


def solution(mesh):
    in_specs = (
        P(None, None, ("grp", "dom")),
        P(None, None, None, ("grp", "dom")),
        P(None, None, None, ("grp", "dom")),
        P(None, None, None, ("grp", "dom")),
        P(),
        P(),
        P(),
        P(None, ("grp", "dom")),
        P(None, ("grp", "dom")),
        P(("grp", "dom")),
    )
    out_specs = P(None, None, ("grp", "dom"))
    return jax.shard_map(local, mesh=mesh, in_specs=in_specs, out_specs=out_specs, check_vma=False)
```

```python
import math

import jax
import jax.numpy as jnp
from jax import lax
from jax.experimental import pallas as pl
from jax.experimental.pallas import tpu as pltpu
from jax.sharding import PartitionSpec as P

ORDER = 6
NB = 56
NQ = 9
NF = 21
FP = 24
E = 128
LN = NQ * E
TR = NQ * FP

F32 = jnp.float32

W_FIRST = [0.5 ** (k + 1) / math.factorial(k + 1) for k in range(ORDER)]
W_LATER = [(1.0 - 0.5 ** (k + 1)) / math.factorial(k + 1) for k in range(ORDER)]


BF = jnp.bfloat16


def _bdot(a, b):
    return jnp.dot(a, b, preferred_element_type=F32)


def _split2(x):
    hi = x.astype(BF)
    return hi, (x - hi.astype(F32)).astype(BF)


def _dot3(a, b):
    return _bdot(a[0], b[0]) + (_bdot(a[0], b[1]) + _bdot(a[1], b[0]))


def _tdot(a, b):
    return lax.dot_general(a, b, (((0,), (0,)), ((), ())), preferred_element_type=F32)


def _dot3_t(a, b):
    return _tdot(a[0], b[0]) + (_tdot(a[0], b[1]) + _tdot(a[1], b[0]))


def _rows84(ref):
    return jnp.concatenate([ref[r] for r in range(NF)], axis=0)


def _split3(x):
    hi = x.astype(BF)
    r = x - hi.astype(F32)
    mid = r.astype(BF)
    return hi, mid, (r - mid.astype(F32)).astype(BF)


def _sel(parts, onehot):
    return (_bdot(parts[0], onehot) + _bdot(parts[1], onehot)) + _bdot(parts[2], onehot)


def _load_field(ref):
    return jnp.concatenate([ref[p] for p in range(NQ)], axis=1)


def _store_field(ref, val):
    for q in range(NQ):
        ref[q] = val[:, q * E:(q + 1) * E]


def _mix_vol(a_ref, star_ref, out_ref, sign):
    for q in range(NQ):
        acc = None
        for p in range(NQ):
            srow = star_ref[p, q]
            for d in range(3):
                t = a_ref[d * NB:(d + 1) * NB, p * E:(p + 1) * E] * srow[d:d + 1, :]
                acc = t if acc is None else acc + t
        out_ref[:, q * E:(q + 1) * E] = acc if sign > 0 else -acc


def _taylor(x, star_ref, stiff_p, d_ref, a_ref, accs):
    for ref, w in accs:
        ref[...] = w[0] * x
    d_ref[...] = x
    for k in range(ORDER - 1):
        a_ref[...] = _dot3(stiff_p, _split2(d_ref[...]))
        _mix_vol(a_ref, star_ref, d_ref, -1)
        dn = d_ref[...]
        for ref, w in accs:
            ref[...] = ref[...] + w[k + 1] * dn


def _table(x, trace_p, yt_ref, t_ref):
    yt = _dot3(trace_p, _split2(x))
    for p in range(NQ):
        yt_ref[p] = yt[:, p * E:(p + 1) * E]
    t_ref[...] = jnp.zeros(t_ref.shape, F32)
    for f in range(4):
        for p in range(NQ):
            t_ref[p * FP:p * FP + NF, f * E:(f + 1) * E] = yt_ref[p, pl.ds(f, NF, stride=4), :]


def _send(tables, send_ref, outs):
    rows = lax.broadcasted_iota(jnp.int32, (4 * E, 3 * E), 0)
    onehot = jnp.where(rows == send_ref[...], 1.0, 0.0).astype(BF)
    s = _sel(_split3(jnp.concatenate(tables, axis=0)), onehot)
    for i, (lo_ref, hi_ref, g_ref) in enumerate(outs):
        blk = s[i * TR:(i + 1) * TR]
        lo_ref[...] = blk[:, 0:E]
        hi_ref[...] = blk[:, E:2 * E]
        g_ref[...] = blk[:, 2 * E:3 * E]


def _gather(comb, slot_ref, face_ref, g_ref):
    rows = lax.broadcasted_iota(jnp.int32, (8 * E, E), 0)
    parts = _split3(comb)
    for f in range(4):
        v = slot_ref[f:f + 1, :]
        nf = face_ref[f:f + 1, :]
        s = v - E
        src = jnp.where(v < E, nf * E + v, 4 * E + s + jnp.where(s >= 2 * E, 64, 0))
        onehot = jnp.where(rows == src, 1.0, 0.0).astype(BF)
        g_ref[:, f * E:(f + 1) * E] = _sel(parts, onehot)


def _lift_parts(lift_ref, lt_ref):
    lt_ref[:, 0:NB] = _rows84(lift_ref)
    return [_split2(lt_ref[pl.ds(f, NF, stride=4), 0:NB]) for f in range(4)]


def _update(b, x, s_ref, g_ref, star_ref, fo_ref, fn_ref, stiff_ref, lift_p, a_ref, v_ref, yf_ref):
    xp = _split2(x)
    for d in range(3):
        a_ref[d * NB:(d + 1) * NB, :] = _dot3_t(_split2(stiff_ref[d]), xp)
    _mix_vol(a_ref, star_ref, v_ref, 1)
    for q in range(NQ):
        accs = [None] * 4
        for p in range(NQ):
            orow = fo_ref[p, q]
            nrow = fn_ref[p, q]
            for f in range(4):
                t = (s_ref[p * FP:(p + 1) * FP, f * E:(f + 1) * E] * orow[f:f + 1, :]
                     + g_ref[p * FP:(p + 1) * FP, f * E:(f + 1) * E] * nrow[f:f + 1, :])
                accs[f] = t if accs[f] is None else accs[f] + t
        for f in range(4):
            yf_ref[f * FP:(f + 1) * FP, q * E:(q + 1) * E] = accs[f]
    ftot = None
    for f in range(4):
        t = _dot3_t(lift_p[f], _split2(yf_ref[f * FP:f * FP + NF, :]))
        ftot = t if ftot is None else ftot + t
    return (b + v_ref[...]) - ftot


def _kernel_a(x_ref, star_ref, stiff_ref, trace_ref, send_ref,
              first_ref, fl_ref, t1_ref, t1l_ref, s1lo, s1hi, s1g, plo, phi, pg, slg,
              d_ref, a_ref, acc1_ref, acc2_ref, tl_ref, yt_ref,
              sllo, slhi):
    x = _load_field(x_ref)
    stiff_st = jnp.concatenate([stiff_ref[d] for d in range(3)], axis=0)
    _taylor(x, star_ref, _split2(stiff_st), d_ref, a_ref, [(acc1_ref, W_FIRST), (acc2_ref, W_LATER)])
    first = acc1_ref[...]
    later = acc2_ref[...]
    _store_field(first_ref, first)
    _store_field(fl_ref, first + later)
    trace_p = _split2(_rows84(trace_ref))
    _table(first, trace_p, yt_ref, t1_ref)
    _table(later, trace_p, yt_ref, tl_ref)
    t1l_ref[...] = t1_ref[...] + tl_ref[...]
    _send([t1_ref[...], tl_ref[...]], send_ref, [(s1lo, s1hi, s1g), (sllo, slhi, slg)])
    plo[...] = s1lo[...] + sllo[...]
    phi[...] = s1hi[...] + slhi[...]
    pg[...] = s1g[...] + slg[...]


def _kernel_b(grp_ref, x_ref, first_ref, fl_ref, t1_ref, t1l_ref, s1g, plo, phi, pg, slg,
              r1lo, r1hi, r1ghi, slot_ref, face_ref, star_ref, fo_ref, fn_ref,
              stiff_ref, lift_ref, trace_ref, send_ref,
              base_ref, integ_ref, own_ref, elo, ehi, egup, egdn,
              d_ref, a_ref, v_ref, yf_ref, g_ref, acc_ref, yt_ref, lt_ref):
    grp = grp_ref[0]

    @pl.when(grp == 0)
    def _():
        comb = jnp.concatenate([t1_ref[...], r1lo[...], r1hi[...], jnp.zeros((TR, E), F32), r1ghi[...]], axis=1)
        _gather(comb, slot_ref, face_ref, g_ref)
        mid = _update(_load_field(x_ref), _load_field(first_ref), t1_ref, g_ref, star_ref, fo_ref, fn_ref,
                      stiff_ref, _lift_parts(lift_ref, lt_ref), a_ref, v_ref, yf_ref)
        _store_field(base_ref, mid)
        stiff_st = jnp.concatenate([stiff_ref[d] for d in range(3)], axis=0)
        _taylor(mid, star_ref, _split2(stiff_st), d_ref, a_ref, [(acc_ref, W_FIRST)])
        second = acc_ref[...]
        _store_field(integ_ref, second)
        _table(second, _split2(_rows84(trace_ref)), yt_ref, own_ref)
        _send([own_ref[...]], send_ref, [(elo, ehi, egdn)])
        egup[...] = s1g[...] + egdn[...]

    @pl.when(grp != 0)
    def _():
        base_ref[...] = x_ref[...]
        integ_ref[...] = fl_ref[...]
        own_ref[...] = t1l_ref[...]
        elo[...] = plo[...]
        ehi[...] = phi[...]
        egup[...] = pg[...]

    @pl.when(grp == 1)
    def _():
        egdn[...] = slg[...]

    @pl.when(grp > 1)
    def _():
        egdn[...] = pg[...]


def _kernel_c(base_ref, integ_ref, own_ref, r2lo, r2hi, r2glo, r2ghi, slot_ref, face_ref,
              star_ref, fo_ref, fn_ref, stiff_ref, lift_ref,
              out_ref, a_ref, v_ref, yf_ref, g_ref, lt_ref):
    comb = jnp.concatenate([own_ref[...], r2lo[...], r2hi[...], r2glo[...], r2ghi[...]], axis=1)
    _gather(comb, slot_ref, face_ref, g_ref)
    out = _update(_load_field(base_ref), _load_field(integ_ref), own_ref, g_ref, star_ref, fo_ref, fn_ref,
                  stiff_ref, _lift_parts(lift_ref, lt_ref), a_ref, v_ref, yf_ref)
    _store_field(out_ref, out)


def _vmem():
    return pl.BlockSpec(memory_space=pltpu.VMEM)


def _smem():
    return pl.BlockSpec(memory_space=pltpu.SMEM)


def _sds(shape):
    return jax.ShapeDtypeStruct(shape, F32)


def exchange(lo, hi, gup, gdn):
    n_dom = lax.axis_size("dom")
    n_grp = lax.axis_size("grp")
    from_lo = lax.ppermute(hi, "dom", [(i, i + 1) for i in range(n_dom - 1)])
    from_hi = lax.ppermute(lo, "dom", [(i + 1, i) for i in range(n_dom - 1)])
    from_glo = lax.ppermute(gup, "grp", [(i, i + 1) for i in range(n_grp - 1)])
    from_ghi = lax.ppermute(gdn, "grp", [(i + 1, i) for i in range(n_grp - 1)])
    return from_lo, from_hi, from_glo, from_ghi


def exchange_fault(lo, hi, g):
    n_dom = lax.axis_size("dom")
    axes = ("grp", "dom")
    from_lo = lax.ppermute(hi, axes, [(i, i + 1) for i in range(n_dom - 1)])
    from_hi = lax.ppermute(lo, axes, [(i + 1, i) for i in range(n_dom - 1)])
    from_ghi = lax.ppermute(g, axes, [(n_dom + i, i) for i in range(n_dom)])
    return from_lo, from_hi, from_ghi


def local(state, star, flux_own, flux_nbr, stiff, trace, lift, nbr_slot, nbr_face, send_slot):
    grp = lax.axis_index("grp").astype(jnp.int32).reshape(1)
    x0 = jnp.transpose(state, (1, 0, 2))
    star = jnp.transpose(star, (1, 2, 0, 3))
    flux_own = jnp.transpose(flux_own, (1, 2, 0, 3))
    flux_nbr = jnp.transpose(flux_nbr, (1, 2, 0, 3))
    trace = jnp.transpose(trace, (1, 0, 2))
    lift = jnp.transpose(lift, (2, 0, 1))
    send = send_slot.reshape(1, 3 * E)

    field = _sds((NQ, NB, E))
    table = _sds((TR, 4 * E))
    part = _sds((TR, E))
    wide = pltpu.VMEM((NB, LN), F32)
    outs_a = pl.pallas_call(
        _kernel_a,
        out_shape=(field, field, table, table) + (part,) * 7,
        in_specs=[_vmem()] * 5,
        out_specs=tuple([_vmem()] * 11),
        scratch_shapes=[wide, pltpu.VMEM((3 * NB, LN), F32), wide, wide, pltpu.VMEM((TR, 4 * E), F32),
                        pltpu.VMEM((NQ, 4 * NF, E), F32), pltpu.VMEM((TR, E), F32), pltpu.VMEM((TR, E), F32)],
    )(x0, star, stiff, trace, send)
    first, fl, t1, t1l, s1lo, s1hi, s1g, plo, phi, pg, slg = outs_a

    r1 = exchange_fault(s1lo, s1hi, s1g)

    outs_b = pl.pallas_call(
        _kernel_b,
        out_shape=(field, field, table, part, part, part, part),
        in_specs=[_smem()] + [_vmem()] * 22,
        out_specs=tuple([_vmem()] * 7),
        scratch_shapes=[wide, pltpu.VMEM((3 * NB, LN), F32), wide, pltpu.VMEM((4 * FP, LN), F32),
                        pltpu.VMEM((TR, 4 * E), F32), wide, pltpu.VMEM((NQ, 4 * NF, E), F32),
                        pltpu.VMEM((4 * NF, E), F32)],
    )(grp, x0, first, fl, t1, t1l, s1g, plo, phi, pg, slg, *r1, nbr_slot, nbr_face, star, flux_own, flux_nbr,
      stiff, lift, trace, send)
    base, integ, own, elo, ehi, egup, egdn = outs_b

    r2 = exchange(elo, ehi, egup, egdn)

    out = pl.pallas_call(
        _kernel_c,
        out_shape=field,
        in_specs=[_vmem()] * 14,
        out_specs=_vmem(),
        scratch_shapes=[pltpu.VMEM((3 * NB, LN), F32), wide, pltpu.VMEM((4 * FP, LN), F32),
                        pltpu.VMEM((TR, 4 * E), F32), pltpu.VMEM((4 * NF, E), F32)],
    )(base, integ, own, *r2, nbr_slot, nbr_face, star, flux_own, flux_nbr, stiff, lift)
    return jnp.transpose(out, (1, 0, 2))


def solution(mesh):
    in_specs = (
        P(None, None, ("grp", "dom")),
        P(None, None, None, ("grp", "dom")),
        P(None, None, None, ("grp", "dom")),
        P(None, None, None, ("grp", "dom")),
        P(),
        P(),
        P(),
        P(None, ("grp", "dom")),
        P(None, ("grp", "dom")),
        P(("grp", "dom")),
    )
    out_specs = P(None, None, ("grp", "dom"))
    return jax.shard_map(local, mesh=mesh, in_specs=in_specs, out_specs=out_specs, check_vma=False)
```

```python
import math

import jax
import jax.numpy as jnp
from jax import lax
from jax.experimental import pallas as pl
from jax.experimental.pallas import tpu as pltpu
from jax.sharding import PartitionSpec as P

ORDER = 6
NB = 56
NQ = 9
NF = 21
FP = 24
E = 128
LN = NQ * E
TR = NQ * FP

F32 = jnp.float32

W_FIRST = [0.5 ** (k + 1) / math.factorial(k + 1) for k in range(ORDER)]
W_LATER = [(1.0 - 0.5 ** (k + 1)) / math.factorial(k + 1) for k in range(ORDER)]


BF = jnp.bfloat16


def _bdot(a, b):
    return jnp.dot(a, b, preferred_element_type=F32)


def _split2(x):
    hi = x.astype(BF)
    return hi, (x - hi.astype(F32)).astype(BF)


def _dot3(a, b):
    return _bdot(a[0], b[0]) + (_bdot(a[0], b[1]) + _bdot(a[1], b[0]))


def _tdot(a, b):
    return lax.dot_general(a, b, (((0,), (0,)), ((), ())), preferred_element_type=F32)


def _dot3_t(a, b):
    return _tdot(a[0], b[0]) + (_tdot(a[0], b[1]) + _tdot(a[1], b[0]))


def _rows84(ref):
    return jnp.concatenate([ref[r] for r in range(NF)], axis=0)


def _split3(x):
    hi = x.astype(BF)
    r = x - hi.astype(F32)
    mid = r.astype(BF)
    return hi, mid, (r - mid.astype(F32)).astype(BF)


def _sel(parts, onehot):
    return (_bdot(parts[0], onehot) + _bdot(parts[1], onehot)) + _bdot(parts[2], onehot)


def _load_field(ref):
    return jnp.concatenate([ref[p] for p in range(NQ)], axis=1)


def _store_field(ref, val):
    for q in range(NQ):
        ref[q] = val[:, q * E:(q + 1) * E]


def _mix_vol(a_ref, star_ref, out_ref, sign):
    for q in range(NQ):
        acc = None
        for p in range(NQ):
            srow = star_ref[p, q]
            for d in range(3):
                t = a_ref[d * NB:(d + 1) * NB, p * E:(p + 1) * E] * srow[d:d + 1, :]
                acc = t if acc is None else acc + t
        out_ref[:, q * E:(q + 1) * E] = acc if sign > 0 else -acc


def _taylor(x, star_ref, stiff_p, d_ref, a_ref, accs):
    for ref, w in accs:
        ref[...] = w[0] * x
    d_ref[...] = x
    for k in range(ORDER - 1):
        a_ref[...] = _dot3(stiff_p, _split2(d_ref[...]))
        _mix_vol(a_ref, star_ref, d_ref, -1)
        dn = d_ref[...]
        for ref, w in accs:
            ref[...] = ref[...] + w[k + 1] * dn


def _table(x, trace_p, yt_ref, t_ref):
    yt = _dot3(trace_p, _split2(x))
    for p in range(NQ):
        yt_ref[p] = yt[:, p * E:(p + 1) * E]
    t_ref[...] = jnp.zeros(t_ref.shape, F32)
    for f in range(4):
        for p in range(NQ):
            t_ref[p * FP:p * FP + NF, f * E:(f + 1) * E] = yt_ref[p, pl.ds(f, NF, stride=4), :]


def _send(tables, send_ref, outs):
    rows = lax.broadcasted_iota(jnp.int32, (4 * E, 3 * E), 0)
    onehot = jnp.where(rows == send_ref[...], 1.0, 0.0).astype(BF)
    s = _sel(_split3(jnp.concatenate(tables, axis=0)), onehot)
    for i, (lo_ref, hi_ref, g_ref) in enumerate(outs):
        blk = s[i * TR:(i + 1) * TR]
        lo_ref[...] = blk[:, 0:E]
        hi_ref[...] = blk[:, E:2 * E]
        g_ref[...] = blk[:, 2 * E:3 * E]


def _gather(comb, slot_ref, face_ref, g_ref, received):
    rows = lax.broadcasted_iota(jnp.int32, (4 * E, E), 0)
    parts = _split3(comb)
    for f in range(4):
        v = slot_ref[f:f + 1, :]
        if received:
            s = v - E
            src = jnp.where(v < E, -1, s + jnp.where(s >= 2 * E, 64, 0))
        else:
            src = jnp.where(v < E, face_ref[f:f + 1, :] * E + v, -1)
        onehot = jnp.where(rows == src, 1.0, 0.0).astype(BF)
        g_ref[:, f * E:(f + 1) * E] = _sel(parts, onehot)


def _fmix(pairs, yf_ref, base_ref=None):
    for q in range(NQ):
        accs = [None] * 4
        for p in range(NQ):
            rows = [fl_ref[p, q] for _, fl_ref in pairs]
            for f in range(4):
                t = None
                for (t_ref, _), row in zip(pairs, rows):
                    u = t_ref[p * FP:(p + 1) * FP, f * E:(f + 1) * E] * row[f:f + 1, :]
                    t = u if t is None else t + u
                accs[f] = t if accs[f] is None else accs[f] + t
        for f in range(4):
            acc = accs[f]
            if base_ref is not None:
                acc = base_ref[f * FP:(f + 1) * FP, q * E:(q + 1) * E] + acc
            yf_ref[f * FP:(f + 1) * FP, q * E:(q + 1) * E] = acc


def _lift_parts(lift_ref, lt_ref):
    lt_ref[:, 0:NB] = _rows84(lift_ref)
    return [_split2(lt_ref[pl.ds(f, NF, stride=4), 0:NB]) for f in range(4)]


def _vol(b, x, star_ref, stiff_ref, a_ref, v_ref):
    xp = _split2(x)
    for d in range(3):
        a_ref[d * NB:(d + 1) * NB, :] = _dot3_t(_split2(stiff_ref[d]), xp)
    _mix_vol(a_ref, star_ref, v_ref, 1)
    return b + v_ref[...]


def _partial(b, x, own_ref, star_ref, fo_ref, fn_ref, stiff_ref, slot_ref, face_ref,
             a_ref, v_ref, g_ref, bv_ref, yp_ref):
    bv_ref[...] = _vol(b, x, star_ref, stiff_ref, a_ref, v_ref)
    _gather(own_ref[...], slot_ref, face_ref, g_ref, False)
    _fmix([(own_ref, fo_ref), (g_ref, fn_ref)], yp_ref)


def _finish(bv_ref, yp_ref, recv, fn_ref, lift_p, slot_ref, face_ref, g_ref, yf_ref):
    _gather(jnp.concatenate(recv, axis=1), slot_ref, face_ref, g_ref, True)
    _fmix([(g_ref, fn_ref)], yf_ref, yp_ref)
    ftot = None
    for f in range(4):
        t = _dot3_t(lift_p[f], _split2(yf_ref[f * FP:f * FP + NF, :]))
        ftot = t if ftot is None else ftot + t
    return bv_ref[...] - ftot


def _kernel_a1(x_ref, star_ref, stiff_ref, trace_ref, send_ref,
               first_ref, later_ref, t1_ref, s1lo, s1hi, s1g,
               d_ref, a_ref, acc1_ref, acc2_ref, yt_ref):
    x = _load_field(x_ref)
    stiff_st = jnp.concatenate([stiff_ref[d] for d in range(3)], axis=0)
    _taylor(x, star_ref, _split2(stiff_st), d_ref, a_ref, [(acc1_ref, W_FIRST), (acc2_ref, W_LATER)])
    first = acc1_ref[...]
    first_ref[...] = first
    later_ref[...] = acc2_ref[...]
    _table(first, _split2(_rows84(trace_ref)), yt_ref, t1_ref)
    _send([t1_ref[...]], send_ref, [(s1lo, s1hi, s1g)])


def _kernel_a2(grp_ref, x_ref, first_ref, later_ref, t1_ref, s1lo, s1hi, s1g, star_ref, fo_ref, fn_ref,
               stiff_ref, trace_ref, send_ref, slot_ref, face_ref,
               fl_ref, t1l_ref, plo, phi, pg, slg, bv_ref, yp_ref,
               tl_ref, yt_ref, sllo, slhi, a_ref, v_ref, g_ref):
    later = later_ref[...]
    fl_ref[...] = first_ref[...] + later
    _table(later, _split2(_rows84(trace_ref)), yt_ref, tl_ref)
    t1l_ref[...] = t1_ref[...] + tl_ref[...]
    _send([tl_ref[...]], send_ref, [(sllo, slhi, slg)])
    plo[...] = s1lo[...] + sllo[...]
    phi[...] = s1hi[...] + slhi[...]
    pg[...] = s1g[...] + slg[...]

    @pl.when(grp_ref[0] == 0)
    def _():
        _partial(_load_field(x_ref), first_ref[...], t1_ref, star_ref, fo_ref, fn_ref, stiff_ref,
                 slot_ref, face_ref, a_ref, v_ref, g_ref, bv_ref, yp_ref)


def _kernel_b(grp_ref, x_ref, fl_ref, t1l_ref, s1g, plo, phi, pg, slg, bv_ref, yp_ref,
              r1lo, r1hi, r1ghi, slot_ref, face_ref, star_ref, fn_ref,
              stiff_ref, lift_ref, trace_ref, send_ref,
              base_ref, integ_ref, own_ref, elo, ehi, egup, egdn,
              d_ref, a_ref, yf_ref, g_ref, acc_ref, yt_ref, lt_ref):
    grp = grp_ref[0]

    @pl.when(grp == 0)
    def _():
        recv = [r1lo[...], r1hi[...], jnp.zeros((TR, E), F32), r1ghi[...]]
        mid = _finish(bv_ref, yp_ref, recv, fn_ref, _lift_parts(lift_ref, lt_ref), slot_ref, face_ref,
                      g_ref, yf_ref)
        base_ref[...] = mid
        stiff_st = jnp.concatenate([stiff_ref[d] for d in range(3)], axis=0)
        _taylor(mid, star_ref, _split2(stiff_st), d_ref, a_ref, [(acc_ref, W_FIRST)])
        second = acc_ref[...]
        integ_ref[...] = second
        _table(second, _split2(_rows84(trace_ref)), yt_ref, own_ref)
        _send([own_ref[...]], send_ref, [(elo, ehi, egdn)])
        egup[...] = s1g[...] + egdn[...]

    @pl.when(grp != 0)
    def _():
        base_ref[...] = _load_field(x_ref)
        integ_ref[...] = fl_ref[...]
        own_ref[...] = t1l_ref[...]
        elo[...] = plo[...]
        ehi[...] = phi[...]
        egup[...] = pg[...]

    @pl.when(grp == 1)
    def _():
        egdn[...] = slg[...]

    @pl.when(grp > 1)
    def _():
        egdn[...] = pg[...]


def _kernel_b2(base_ref, integ_ref, own_ref, star_ref, fo_ref, fn_ref, stiff_ref, slot_ref, face_ref,
               bv_ref, yp_ref, a_ref, v_ref, g_ref):
    _partial(base_ref[...], integ_ref[...], own_ref, star_ref, fo_ref, fn_ref, stiff_ref,
             slot_ref, face_ref, a_ref, v_ref, g_ref, bv_ref, yp_ref)


def _kernel_c(bv_ref, yp_ref, r2lo, r2hi, r2glo, r2ghi, slot_ref, face_ref, fn_ref, lift_ref,
              out_ref, yf_ref, g_ref, lt_ref):
    recv = [r2lo[...], r2hi[...], r2glo[...], r2ghi[...]]
    out = _finish(bv_ref, yp_ref, recv, fn_ref, _lift_parts(lift_ref, lt_ref), slot_ref, face_ref,
                  g_ref, yf_ref)
    _store_field(out_ref, out)


def _vmem():
    return pl.BlockSpec(memory_space=pltpu.VMEM)


def _smem():
    return pl.BlockSpec(memory_space=pltpu.SMEM)


def _sds(shape):
    return jax.ShapeDtypeStruct(shape, F32)


def exchange(lo, hi, gup, gdn):
    n_dom = lax.axis_size("dom")
    n_grp = lax.axis_size("grp")
    from_lo = lax.ppermute(hi, "dom", [(i, i + 1) for i in range(n_dom - 1)])
    from_hi = lax.ppermute(lo, "dom", [(i + 1, i) for i in range(n_dom - 1)])
    from_glo = lax.ppermute(gup, "grp", [(i, i + 1) for i in range(n_grp - 1)])
    from_ghi = lax.ppermute(gdn, "grp", [(i + 1, i) for i in range(n_grp - 1)])
    return from_lo, from_hi, from_glo, from_ghi


def exchange_fault(lo, hi, g):
    n_dom = lax.axis_size("dom")
    axes = ("grp", "dom")
    from_lo = lax.ppermute(hi, axes, [(i, i + 1) for i in range(n_dom - 1)])
    from_hi = lax.ppermute(lo, axes, [(i + 1, i) for i in range(n_dom - 1)])
    from_ghi = lax.ppermute(g, axes, [(n_dom + i, i) for i in range(n_dom)])
    return from_lo, from_hi, from_ghi


def local(state, star, flux_own, flux_nbr, stiff, trace, lift, nbr_slot, nbr_face, send_slot):
    grp = lax.axis_index("grp").astype(jnp.int32).reshape(1)
    x0 = jnp.transpose(state, (1, 0, 2))
    star = jnp.transpose(star, (1, 2, 0, 3))
    flux_own = jnp.transpose(flux_own, (1, 2, 0, 3))
    flux_nbr = jnp.transpose(flux_nbr, (1, 2, 0, 3))
    trace = jnp.transpose(trace, (1, 0, 2))
    lift = jnp.transpose(lift, (2, 0, 1))
    send = send_slot.reshape(1, 3 * E)

    field = _sds((NQ, NB, E))
    flat = _sds((NB, LN))
    table = _sds((TR, 4 * E))
    part = _sds((TR, E))
    yflux = _sds((4 * FP, LN))
    wide = pltpu.VMEM((NB, LN), F32)
    amat = pltpu.VMEM((3 * NB, LN), F32)
    tab = pltpu.VMEM((TR, 4 * E), F32)
    ytr = pltpu.VMEM((NQ, 4 * NF, E), F32)
    yfs = pltpu.VMEM((4 * FP, LN), F32)
    lts = pltpu.VMEM((4 * NF, E), F32)

    first, later, t1, s1lo, s1hi, s1g = pl.pallas_call(
        _kernel_a1,
        out_shape=(flat, flat, table, part, part, part),
        in_specs=[_vmem()] * 5,
        out_specs=tuple([_vmem()] * 6),
        scratch_shapes=[wide, amat, wide, wide, ytr],
    )(x0, star, stiff, trace, send)

    r1 = exchange_fault(s1lo, s1hi, s1g)

    fl, t1l, plo, phi, pg, slg, bv1, yp1 = pl.pallas_call(
        _kernel_a2,
        out_shape=(flat, table, part, part, part, part, flat, yflux),
        in_specs=[_smem()] + [_vmem()] * 15,
        out_specs=tuple([_vmem()] * 8),
        scratch_shapes=[tab, ytr, pltpu.VMEM((TR, E), F32), pltpu.VMEM((TR, E), F32), amat, wide, tab],
    )(grp, x0, first, later, t1, s1lo, s1hi, s1g, star, flux_own, flux_nbr, stiff, trace, send,
      nbr_slot, nbr_face)

    base, integ, own, elo, ehi, egup, egdn = pl.pallas_call(
        _kernel_b,
        out_shape=(flat, flat, table, part, part, part, part),
        in_specs=[_smem()] + [_vmem()] * 21,
        out_specs=tuple([_vmem()] * 7),
        scratch_shapes=[wide, amat, yfs, tab, wide, ytr, lts],
    )(grp, x0, fl, t1l, s1g, plo, phi, pg, slg, bv1, yp1, *r1, nbr_slot, nbr_face, star, flux_nbr,
      stiff, lift, trace, send)

    r2 = exchange(elo, ehi, egup, egdn)

    bv2, yp2 = pl.pallas_call(
        _kernel_b2,
        out_shape=(flat, yflux),
        in_specs=[_vmem()] * 9,
        out_specs=(_vmem(), _vmem()),
        scratch_shapes=[amat, wide, tab],
    )(base, integ, own, star, flux_own, flux_nbr, stiff, nbr_slot, nbr_face)

    out = pl.pallas_call(
        _kernel_c,
        out_shape=field,
        in_specs=[_vmem()] * 10,
        out_specs=_vmem(),
        scratch_shapes=[yfs, tab, lts],
    )(bv2, yp2, *r2, nbr_slot, nbr_face, flux_nbr, lift)
    return jnp.transpose(out, (1, 0, 2))


def solution(mesh):
    in_specs = (
        P(None, None, ("grp", "dom")),
        P(None, None, None, ("grp", "dom")),
        P(None, None, None, ("grp", "dom")),
        P(None, None, None, ("grp", "dom")),
        P(),
        P(),
        P(),
        P(None, ("grp", "dom")),
        P(None, ("grp", "dom")),
        P(("grp", "dom")),
    )
    out_specs = P(None, None, ("grp", "dom"))
    return jax.shard_map(local, mesh=mesh, in_specs=in_specs, out_specs=out_specs, check_vma=False)
```

```python
import math

import jax
import jax.numpy as jnp
from jax import lax
from jax.experimental import pallas as pl
from jax.experimental.pallas import tpu as pltpu
from jax.sharding import PartitionSpec as P

ORDER = 6
NB = 56
NQ = 9
NF = 21
FP = 24
E = 128
LN = NQ * E
TR = NQ * FP

F32 = jnp.float32

W_FIRST = [0.5 ** (k + 1) / math.factorial(k + 1) for k in range(ORDER)]
W_LATER = [(1.0 - 0.5 ** (k + 1)) / math.factorial(k + 1) for k in range(ORDER)]


BF = jnp.bfloat16


def _bdot(a, b):
    return jnp.dot(a, b, preferred_element_type=F32)


def _split2(x):
    hi = x.astype(BF)
    return hi, (x - hi.astype(F32)).astype(BF)


def _dot3(a, b):
    return _bdot(a[0], b[0]) + (_bdot(a[0], b[1]) + _bdot(a[1], b[0]))


def _tdot(a, b):
    return lax.dot_general(a, b, (((0,), (0,)), ((), ())), preferred_element_type=F32)


def _dot3_t(a, b):
    return _tdot(a[0], b[0]) + (_tdot(a[0], b[1]) + _tdot(a[1], b[0]))


def _rows84(ref):
    return jnp.concatenate([ref[r] for r in range(NF)], axis=0)


def _split3(x):
    hi = x.astype(BF)
    r = x - hi.astype(F32)
    mid = r.astype(BF)
    return hi, mid, (r - mid.astype(F32)).astype(BF)


def _sel(parts, onehot):
    return (_bdot(parts[0], onehot) + _bdot(parts[1], onehot)) + _bdot(parts[2], onehot)


def _load_field(ref):
    return jnp.concatenate([ref[p] for p in range(NQ)], axis=1)


def _store_field(ref, val):
    for q in range(NQ):
        ref[q] = val[:, q * E:(q + 1) * E]


def _mix_vol(a_ref, star_ref, out_ref, sign):
    for q in range(NQ):
        acc = None
        for p in range(NQ):
            srow = star_ref[p, q]
            for d in range(3):
                t = a_ref[d * NB:(d + 1) * NB, p * E:(p + 1) * E] * srow[d:d + 1, :]
                acc = t if acc is None else acc + t
        out_ref[:, q * E:(q + 1) * E] = acc if sign > 0 else -acc


def _taylor(x, star_ref, stiff_p, d_ref, a_ref, accs):
    for ref, w in accs:
        ref[...] = w[0] * x
    d_ref[...] = x
    for k in range(ORDER - 1):
        a_ref[...] = _dot3(stiff_p, _split2(d_ref[...]))
        _mix_vol(a_ref, star_ref, d_ref, -1)
        dn = d_ref[...]
        for ref, w in accs:
            ref[...] = ref[...] + w[k + 1] * dn


def _table(x, trace_p, yt_ref, t_ref):
    yt = _dot3(trace_p, _split2(x))
    for p in range(NQ):
        yt_ref[p] = yt[:, p * E:(p + 1) * E]
    t_ref[...] = jnp.zeros(t_ref.shape, F32)
    for f in range(4):
        for p in range(NQ):
            t_ref[p * FP:p * FP + NF, f * E:(f + 1) * E] = yt_ref[p, pl.ds(f, NF, stride=4), :]


def _send(tables, send_ref, outs):
    rows = lax.broadcasted_iota(jnp.int32, (4 * E, 3 * E), 0)
    onehot = jnp.where(rows == send_ref[...].reshape(1, 3 * E), 1.0, 0.0).astype(BF)
    s = _sel(_split3(jnp.concatenate(tables, axis=0)), onehot)
    for i, (lo_ref, hi_ref, g_ref) in enumerate(outs):
        blk = s[i * TR:(i + 1) * TR]
        lo_ref[...] = blk[:, 0:E]
        hi_ref[...] = blk[:, E:2 * E]
        g_ref[...] = blk[:, 2 * E:3 * E]


def _gather(comb, slot_ref, face_ref, g_ref, received):
    rows = lax.broadcasted_iota(jnp.int32, (4 * E, E), 0)
    parts = _split3(comb)
    for f in range(4):
        v = slot_ref[f:f + 1, :]
        if received:
            s = v - E
            src = jnp.where(v < E, -1, s + jnp.where(s >= 2 * E, 64, 0))
        else:
            src = jnp.where(v < E, face_ref[f:f + 1, :] * E + v, -1)
        onehot = jnp.where(rows == src, 1.0, 0.0).astype(BF)
        g_ref[:, f * E:(f + 1) * E] = _sel(parts, onehot)


def _fmix(pairs, yf_ref, base_ref=None):
    for q in range(NQ):
        accs = [None] * 4
        for p in range(NQ):
            rows = [fl_ref[p, q] for _, fl_ref in pairs]
            for f in range(4):
                t = None
                for (t_ref, _), row in zip(pairs, rows):
                    u = t_ref[p * FP:(p + 1) * FP, f * E:(f + 1) * E] * row[f:f + 1, :]
                    t = u if t is None else t + u
                accs[f] = t if accs[f] is None else accs[f] + t
        for f in range(4):
            acc = accs[f]
            if base_ref is not None:
                acc = base_ref[f * FP:(f + 1) * FP, q * E:(q + 1) * E] + acc
            yf_ref[f * FP:(f + 1) * FP, q * E:(q + 1) * E] = acc


def _lift_parts(lift_ref, lt_ref):
    lt_ref[:, 0:NB] = _rows84(lift_ref)
    return [_split2(lt_ref[pl.ds(f, NF, stride=4), 0:NB]) for f in range(4)]


def _vol(b, x, star_ref, stiff_ref, a_ref, v_ref):
    xp = _split2(x)
    for d in range(3):
        a_ref[d * NB:(d + 1) * NB, :] = _dot3_t(_split2(stiff_ref[d]), xp)
    _mix_vol(a_ref, star_ref, v_ref, 1)
    return b + v_ref[...]


def _partial(b, x, own_ref, star_ref, fo_ref, fn_ref, stiff_ref, slot_ref, face_ref,
             a_ref, v_ref, g_ref, bv_ref, yp_ref):
    bv_ref[...] = _vol(b, x, star_ref, stiff_ref, a_ref, v_ref)
    _gather(own_ref[...], slot_ref, face_ref, g_ref, False)
    _fmix([(own_ref, fo_ref), (g_ref, fn_ref)], yp_ref)


def _finish(bv_ref, yp_ref, recv, fn_ref, lift_p, slot_ref, face_ref, g_ref, yf_ref):
    _gather(jnp.concatenate(recv, axis=1), slot_ref, face_ref, g_ref, True)
    _fmix([(g_ref, fn_ref)], yf_ref, yp_ref)
    ftot = None
    for f in range(4):
        t = _dot3_t(lift_p[f], _split2(yf_ref[f * FP:f * FP + NF, :]))
        ftot = t if ftot is None else ftot + t
    return bv_ref[...] - ftot


def _kernel_a1(x_ref, star_ref, stiff_ref, trace_ref, send_ref,
               first_ref, later_ref, t1_ref, s1lo, s1hi, s1g,
               d_ref, a_ref, acc1_ref, acc2_ref, yt_ref):
    x = _load_field(x_ref)
    stiff_st = jnp.concatenate([stiff_ref[d] for d in range(3)], axis=0)
    _taylor(x, star_ref, _split2(stiff_st), d_ref, a_ref, [(acc1_ref, W_FIRST), (acc2_ref, W_LATER)])
    first = acc1_ref[...]
    first_ref[...] = first
    later_ref[...] = acc2_ref[...]
    _table(first, _split2(_rows84(trace_ref)), yt_ref, t1_ref)
    _send([t1_ref[...]], send_ref, [(s1lo, s1hi, s1g)])


def _kernel_a2(grp_ref, x_ref, first_ref, later_ref, t1_ref, s1lo, s1hi, s1g, star_ref, fo_ref, fn_ref,
               stiff_ref, trace_ref, send_ref, slot_ref, face_ref,
               fl_ref, t1l_ref, plo, phi, pg, slg, bv_ref, yp_ref,
               tl_ref, yt_ref, sllo, slhi, a_ref, v_ref, g_ref):
    @pl.when(grp_ref[0] != 0)
    def _():
        later = later_ref[...]
        fl_ref[...] = first_ref[...] + later
        _table(later, _split2(_rows84(trace_ref)), yt_ref, tl_ref)
        t1l_ref[...] = t1_ref[...] + tl_ref[...]
        _send([tl_ref[...]], send_ref, [(sllo, slhi, slg)])
        plo[...] = s1lo[...] + sllo[...]
        phi[...] = s1hi[...] + slhi[...]
        pg[...] = s1g[...] + slg[...]

    @pl.when(grp_ref[0] == 0)
    def _():
        _partial(_load_field(x_ref), first_ref[...], t1_ref, star_ref, fo_ref, fn_ref, stiff_ref,
                 slot_ref, face_ref, a_ref, v_ref, g_ref, bv_ref, yp_ref)


def _kernel_b(grp_ref, x_ref, fl_ref, t1l_ref, s1g, plo, phi, pg, slg, bv_ref, yp_ref,
              r1lo, r1hi, r1ghi, slot_ref, face_ref, star_ref, fn_ref,
              stiff_ref, lift_ref, trace_ref, send_ref,
              base_ref, integ_ref, own_ref, elo, ehi, egup, egdn,
              d_ref, a_ref, yf_ref, g_ref, acc_ref, yt_ref, lt_ref):
    grp = grp_ref[0]

    @pl.when(grp == 0)
    def _():
        recv = [r1lo[...], r1hi[...], jnp.zeros((TR, E), F32), r1ghi[...]]
        mid = _finish(bv_ref, yp_ref, recv, fn_ref, _lift_parts(lift_ref, lt_ref), slot_ref, face_ref,
                      g_ref, yf_ref)
        base_ref[...] = mid
        stiff_st = jnp.concatenate([stiff_ref[d] for d in range(3)], axis=0)
        _taylor(mid, star_ref, _split2(stiff_st), d_ref, a_ref, [(acc_ref, W_FIRST)])
        second = acc_ref[...]
        integ_ref[...] = second
        _table(second, _split2(_rows84(trace_ref)), yt_ref, own_ref)
        _send([own_ref[...]], send_ref, [(elo, ehi, egdn)])
        egup[...] = s1g[...] + egdn[...]

    @pl.when(grp != 0)
    def _():
        base_ref[...] = _load_field(x_ref)
        integ_ref[...] = fl_ref[...]
        own_ref[...] = t1l_ref[...]
        elo[...] = plo[...]
        ehi[...] = phi[...]
        egup[...] = pg[...]

    @pl.when(grp == 1)
    def _():
        egdn[...] = slg[...]

    @pl.when(grp > 1)
    def _():
        egdn[...] = pg[...]


def _kernel_b2(base_ref, integ_ref, own_ref, star_ref, fo_ref, fn_ref, stiff_ref, slot_ref, face_ref,
               bv_ref, yp_ref, a_ref, v_ref, g_ref):
    _partial(base_ref[...], integ_ref[...], own_ref, star_ref, fo_ref, fn_ref, stiff_ref,
             slot_ref, face_ref, a_ref, v_ref, g_ref, bv_ref, yp_ref)


def _kernel_c(bv_ref, yp_ref, r2lo, r2hi, r2glo, r2ghi, slot_ref, face_ref, fn_ref, lift_ref,
              out_ref, yf_ref, g_ref, lt_ref):
    recv = [r2lo[...], r2hi[...], r2glo[...], r2ghi[...]]
    out = _finish(bv_ref, yp_ref, recv, fn_ref, _lift_parts(lift_ref, lt_ref), slot_ref, face_ref,
                  g_ref, yf_ref)
    _store_field(out_ref, out)


def _vmem():
    return pl.BlockSpec(memory_space=pltpu.VMEM)


def _smem():
    return pl.BlockSpec(memory_space=pltpu.SMEM)


def _sds(shape):
    return jax.ShapeDtypeStruct(shape, F32)


def exchange(lo, hi, gup, gdn):
    n_dom = lax.axis_size("dom")
    n_grp = lax.axis_size("grp")
    from_lo = lax.ppermute(hi, "dom", [(i, i + 1) for i in range(n_dom - 1)])
    from_hi = lax.ppermute(lo, "dom", [(i + 1, i) for i in range(n_dom - 1)])
    from_glo = lax.ppermute(gup, "grp", [(i, i + 1) for i in range(n_grp - 1)])
    from_ghi = lax.ppermute(gdn, "grp", [(i + 1, i) for i in range(n_grp - 1)])
    return from_lo, from_hi, from_glo, from_ghi


def exchange_fault(lo, hi, g):
    n_dom = lax.axis_size("dom")
    axes = ("grp", "dom")
    from_lo = lax.ppermute(hi, axes, [(i, i + 1) for i in range(n_dom - 1)])
    from_hi = lax.ppermute(lo, axes, [(i + 1, i) for i in range(n_dom - 1)])
    from_ghi = lax.ppermute(g, axes, [(n_dom + i, i) for i in range(n_dom)])
    return from_lo, from_hi, from_ghi


def local(state, star, flux_own, flux_nbr, stiff, trace, lift, nbr_slot, nbr_face, send_slot):
    grp = lax.axis_index("grp").astype(jnp.int32).reshape(1)
    x0 = jnp.transpose(state, (1, 0, 2))
    star = jnp.transpose(star, (1, 2, 0, 3))
    flux_own = jnp.transpose(flux_own, (1, 2, 0, 3))
    flux_nbr = jnp.transpose(flux_nbr, (1, 2, 0, 3))
    trace = jnp.transpose(trace, (1, 0, 2))
    lift = jnp.transpose(lift, (2, 0, 1))
    send = send_slot

    field = _sds((NQ, NB, E))
    flat = _sds((NB, LN))
    table = _sds((TR, 4 * E))
    part = _sds((TR, E))
    yflux = _sds((4 * FP, LN))
    wide = pltpu.VMEM((NB, LN), F32)
    amat = pltpu.VMEM((3 * NB, LN), F32)
    tab = pltpu.VMEM((TR, 4 * E), F32)
    ytr = pltpu.VMEM((NQ, 4 * NF, E), F32)
    yfs = pltpu.VMEM((4 * FP, LN), F32)
    lts = pltpu.VMEM((4 * NF, E), F32)

    first, later, t1, s1lo, s1hi, s1g = pl.pallas_call(
        _kernel_a1,
        out_shape=(flat, flat, table, part, part, part),
        in_specs=[_vmem()] * 5,
        out_specs=tuple([_vmem()] * 6),
        scratch_shapes=[wide, amat, wide, wide, ytr],
    )(x0, star, stiff, trace, send)

    r1 = exchange_fault(s1lo, s1hi, s1g)

    fl, t1l, plo, phi, pg, slg, bv1, yp1 = pl.pallas_call(
        _kernel_a2,
        out_shape=(flat, table, part, part, part, part, flat, yflux),
        in_specs=[_smem()] + [_vmem()] * 15,
        out_specs=tuple([_vmem()] * 8),
        scratch_shapes=[tab, ytr, pltpu.VMEM((TR, E), F32), pltpu.VMEM((TR, E), F32), amat, wide, tab],
    )(grp, x0, first, later, t1, s1lo, s1hi, s1g, star, flux_own, flux_nbr, stiff, trace, send,
      nbr_slot, nbr_face)

    base, integ, own, elo, ehi, egup, egdn = pl.pallas_call(
        _kernel_b,
        out_shape=(flat, flat, table, part, part, part, part),
        in_specs=[_smem()] + [_vmem()] * 21,
        out_specs=tuple([_vmem()] * 7),
        scratch_shapes=[wide, amat, yfs, tab, wide, ytr, lts],
    )(grp, x0, fl, t1l, s1g, plo, phi, pg, slg, bv1, yp1, *r1, nbr_slot, nbr_face, star, flux_nbr,
      stiff, lift, trace, send)

    r2 = exchange(elo, ehi, egup, egdn)

    bv2, yp2 = pl.pallas_call(
        _kernel_b2,
        out_shape=(flat, yflux),
        in_specs=[_vmem()] * 9,
        out_specs=(_vmem(), _vmem()),
        scratch_shapes=[amat, wide, tab],
    )(base, integ, own, star, flux_own, flux_nbr, stiff, nbr_slot, nbr_face)

    out = pl.pallas_call(
        _kernel_c,
        out_shape=field,
        in_specs=[_vmem()] * 10,
        out_specs=_vmem(),
        scratch_shapes=[yfs, tab, lts],
    )(bv2, yp2, *r2, nbr_slot, nbr_face, flux_nbr, lift)
    return jnp.transpose(out, (1, 0, 2))


def solution(mesh):
    in_specs = (
        P(None, None, ("grp", "dom")),
        P(None, None, None, ("grp", "dom")),
        P(None, None, None, ("grp", "dom")),
        P(None, None, None, ("grp", "dom")),
        P(),
        P(),
        P(),
        P(None, ("grp", "dom")),
        P(None, ("grp", "dom")),
        P(("grp", "dom")),
    )
    out_specs = P(None, None, ("grp", "dom"))
    return jax.shard_map(local, mesh=mesh, in_specs=in_specs, out_specs=out_specs, check_vma=False)
```

```python
import math

import jax
import jax.numpy as jnp
from jax import lax
from jax.experimental import pallas as pl
from jax.experimental.pallas import tpu as pltpu
from jax.sharding import PartitionSpec as P

ORDER = 6
NB = 56
NQ = 9
NF = 21
FP = 24
E = 128
LN = NQ * E
TR = NQ * FP

F32 = jnp.float32

W_FIRST = [0.5 ** (k + 1) / math.factorial(k + 1) for k in range(ORDER)]
W_LATER = [(1.0 - 0.5 ** (k + 1)) / math.factorial(k + 1) for k in range(ORDER)]


BF = jnp.bfloat16


def _bdot(a, b):
    return jnp.dot(a, b, preferred_element_type=F32)


def _split2(x):
    hi = x.astype(BF)
    return hi, (x - hi.astype(F32)).astype(BF)


def _dot3(a, b):
    return _bdot(a[0], b[0]) + (_bdot(a[0], b[1]) + _bdot(a[1], b[0]))


def _tdot(a, b):
    return lax.dot_general(a, b, (((0,), (0,)), ((), ())), preferred_element_type=F32)


def _dot3_t(a, b):
    return _tdot(a[0], b[0]) + (_tdot(a[0], b[1]) + _tdot(a[1], b[0]))


def _rows84(ref):
    return jnp.concatenate([ref[r] for r in range(NF)], axis=0)


def _lhs3(a):
    h, l = _split2(jnp.concatenate([a, jnp.zeros((a.shape[0], 8), F32)], axis=1))
    return jnp.concatenate([h, h, l], axis=1)


def _rhs3(x):
    h, l = _split2(jnp.concatenate([x, jnp.zeros((8, x.shape[1]), F32)], axis=0))
    return jnp.concatenate([h, l, h], axis=0)


def _split3(x):
    hi = x.astype(BF)
    r = x - hi.astype(F32)
    mid = r.astype(BF)
    return hi, mid, (r - mid.astype(F32)).astype(BF)


def _sel(parts, onehot):
    return (_bdot(parts[0], onehot) + _bdot(parts[1], onehot)) + _bdot(parts[2], onehot)


def _load_field(ref):
    return jnp.concatenate([ref[p] for p in range(NQ)], axis=1)


def _store_field(ref, val):
    for q in range(NQ):
        ref[q] = val[:, q * E:(q + 1) * E]


def _mix_vol(a_ref, star_ref, out_ref, sign):
    for q in range(NQ):
        acc = None
        for p in range(NQ):
            srow = star_ref[p, q]
            for d in range(3):
                t = a_ref[d * NB:(d + 1) * NB, p * E:(p + 1) * E] * srow[d:d + 1, :]
                acc = t if acc is None else acc + t
        out_ref[:, q * E:(q + 1) * E] = acc if sign > 0 else -acc


def _taylor(x, star_ref, stiff_p, d_ref, a_ref, accs):
    for ref, w in accs:
        ref[...] = w[0] * x
    d_ref[...] = x
    for k in range(ORDER - 1):
        a_ref[...] = _bdot(stiff_p, _rhs3(d_ref[...]))
        _mix_vol(a_ref, star_ref, d_ref, -1)
        dn = d_ref[...]
        for ref, w in accs:
            ref[...] = ref[...] + w[k + 1] * dn


def _table(x, trace_p, yt_ref, t_ref):
    yt = _bdot(trace_p, _rhs3(x))
    for p in range(NQ):
        yt_ref[p] = yt[:, p * E:(p + 1) * E]
    t_ref[...] = jnp.zeros(t_ref.shape, F32)
    for f in range(4):
        for p in range(NQ):
            t_ref[p * FP:p * FP + NF, f * E:(f + 1) * E] = yt_ref[p, pl.ds(f, NF, stride=4), :]


def _send(tables, send_ref, outs):
    rows = lax.broadcasted_iota(jnp.int32, (4 * E, 3 * E), 0)
    onehot = jnp.where(rows == send_ref[...].reshape(1, 3 * E), 1.0, 0.0).astype(BF)
    s = _sel(_split3(jnp.concatenate(tables, axis=0)), onehot)
    for i, (lo_ref, hi_ref, g_ref) in enumerate(outs):
        blk = s[i * TR:(i + 1) * TR]
        lo_ref[...] = blk[:, 0:E]
        hi_ref[...] = blk[:, E:2 * E]
        g_ref[...] = blk[:, 2 * E:3 * E]


def _gather(comb, slot_ref, face_ref, g_ref, received):
    rows = lax.broadcasted_iota(jnp.int32, (4 * E, E), 0)
    parts = _split3(comb)
    for f in range(4):
        v = slot_ref[f:f + 1, :]
        if received:
            s = v - E
            src = jnp.where(v < E, -1, s + jnp.where(s >= 2 * E, 64, 0))
        else:
            src = jnp.where(v < E, face_ref[f:f + 1, :] * E + v, -1)
        onehot = jnp.where(rows == src, 1.0, 0.0).astype(BF)
        g_ref[:, f * E:(f + 1) * E] = _sel(parts, onehot)


def _fmix(pairs, yf_ref, base_ref=None):
    for q in range(NQ):
        accs = [None] * 4
        for p in range(NQ):
            rows = [fl_ref[p, q] for _, fl_ref in pairs]
            for f in range(4):
                t = None
                for (t_ref, _), row in zip(pairs, rows):
                    u = t_ref[p * FP:(p + 1) * FP, f * E:(f + 1) * E] * row[f:f + 1, :]
                    t = u if t is None else t + u
                accs[f] = t if accs[f] is None else accs[f] + t
        for f in range(4):
            acc = accs[f]
            if base_ref is not None:
                acc = base_ref[f * FP:(f + 1) * FP, q * E:(q + 1) * E] + acc
            yf_ref[f * FP:(f + 1) * FP, q * E:(q + 1) * E] = acc


def _lift_parts(lift_ref, lt_ref):
    lt_ref[:, 0:NB] = _rows84(lift_ref)
    return [_split2(lt_ref[pl.ds(f, NF, stride=4), 0:NB]) for f in range(4)]


def _vol(b, x, star_ref, stiff_ref, a_ref, v_ref):
    xp = _split2(x)
    for d in range(3):
        a_ref[d * NB:(d + 1) * NB, :] = _dot3_t(_split2(stiff_ref[d]), xp)
    _mix_vol(a_ref, star_ref, v_ref, 1)
    return b + v_ref[...]


def _partial(b, x, own_ref, star_ref, fo_ref, fn_ref, stiff_ref, slot_ref, face_ref,
             a_ref, v_ref, g_ref, bv_ref, yp_ref):
    bv_ref[...] = _vol(b, x, star_ref, stiff_ref, a_ref, v_ref)
    _gather(own_ref[...], slot_ref, face_ref, g_ref, False)
    _fmix([(own_ref, fo_ref), (g_ref, fn_ref)], yp_ref)


def _finish(bv_ref, yp_ref, recv, fn_ref, lift_p, slot_ref, face_ref, g_ref, yf_ref):
    _gather(jnp.concatenate(recv, axis=1), slot_ref, face_ref, g_ref, True)
    _fmix([(g_ref, fn_ref)], yf_ref, yp_ref)
    ftot = None
    for f in range(4):
        t = _dot3_t(lift_p[f], _split2(yf_ref[f * FP:f * FP + NF, :]))
        ftot = t if ftot is None else ftot + t
    return bv_ref[...] - ftot


def _kernel_a1(x_ref, star_ref, stiff_ref, trace_ref, send_ref,
               first_ref, later_ref, t1_ref, s1lo, s1hi, s1g,
               d_ref, a_ref, acc1_ref, acc2_ref, yt_ref):
    x = _load_field(x_ref)
    stiff_st = jnp.concatenate([stiff_ref[d] for d in range(3)], axis=0)
    _taylor(x, star_ref, _lhs3(stiff_st), d_ref, a_ref, [(acc1_ref, W_FIRST), (acc2_ref, W_LATER)])
    first = acc1_ref[...]
    first_ref[...] = first
    later_ref[...] = acc2_ref[...]
    _table(first, _lhs3(_rows84(trace_ref)), yt_ref, t1_ref)
    _send([t1_ref[...]], send_ref, [(s1lo, s1hi, s1g)])


def _kernel_a2(grp_ref, x_ref, first_ref, later_ref, t1_ref, s1lo, s1hi, s1g, star_ref, fo_ref, fn_ref,
               stiff_ref, trace_ref, send_ref, slot_ref, face_ref,
               fl_ref, t1l_ref, plo, phi, pg, slg, bv_ref, yp_ref,
               tl_ref, yt_ref, sllo, slhi, a_ref, v_ref, g_ref):
    @pl.when(grp_ref[0] != 0)
    def _():
        later = later_ref[...]
        fl_ref[...] = first_ref[...] + later
        _table(later, _lhs3(_rows84(trace_ref)), yt_ref, tl_ref)
        t1l_ref[...] = t1_ref[...] + tl_ref[...]
        _send([tl_ref[...]], send_ref, [(sllo, slhi, slg)])
        plo[...] = s1lo[...] + sllo[...]
        phi[...] = s1hi[...] + slhi[...]
        pg[...] = s1g[...] + slg[...]

    @pl.when(grp_ref[0] == 0)
    def _():
        _partial(_load_field(x_ref), first_ref[...], t1_ref, star_ref, fo_ref, fn_ref, stiff_ref,
                 slot_ref, face_ref, a_ref, v_ref, g_ref, bv_ref, yp_ref)


def _kernel_b(grp_ref, x_ref, fl_ref, t1l_ref, s1g, plo, phi, pg, slg, bv_ref, yp_ref,
              r1lo, r1hi, r1ghi, slot_ref, face_ref, star_ref, fn_ref,
              stiff_ref, lift_ref, trace_ref, send_ref,
              base_ref, integ_ref, own_ref, elo, ehi, egup, egdn,
              d_ref, a_ref, yf_ref, g_ref, acc_ref, yt_ref, lt_ref):
    grp = grp_ref[0]

    @pl.when(grp == 0)
    def _():
        recv = [r1lo[...], r1hi[...], jnp.zeros((TR, E), F32), r1ghi[...]]
        mid = _finish(bv_ref, yp_ref, recv, fn_ref, _lift_parts(lift_ref, lt_ref), slot_ref, face_ref,
                      g_ref, yf_ref)
        base_ref[...] = mid
        stiff_st = jnp.concatenate([stiff_ref[d] for d in range(3)], axis=0)
        _taylor(mid, star_ref, _lhs3(stiff_st), d_ref, a_ref, [(acc_ref, W_FIRST)])
        second = acc_ref[...]
        integ_ref[...] = second
        _table(second, _lhs3(_rows84(trace_ref)), yt_ref, own_ref)
        _send([own_ref[...]], send_ref, [(elo, ehi, egdn)])
        egup[...] = s1g[...] + egdn[...]

    @pl.when(grp != 0)
    def _():
        base_ref[...] = _load_field(x_ref)
        integ_ref[...] = fl_ref[...]
        own_ref[...] = t1l_ref[...]
        elo[...] = plo[...]
        ehi[...] = phi[...]
        egup[...] = pg[...]

    @pl.when(grp == 1)
    def _():
        egdn[...] = slg[...]

    @pl.when(grp > 1)
    def _():
        egdn[...] = pg[...]


def _kernel_b2(base_ref, integ_ref, own_ref, star_ref, fo_ref, fn_ref, stiff_ref, slot_ref, face_ref,
               bv_ref, yp_ref, a_ref, v_ref, g_ref):
    _partial(base_ref[...], integ_ref[...], own_ref, star_ref, fo_ref, fn_ref, stiff_ref,
             slot_ref, face_ref, a_ref, v_ref, g_ref, bv_ref, yp_ref)


def _kernel_c(bv_ref, yp_ref, r2lo, r2hi, r2glo, r2ghi, slot_ref, face_ref, fn_ref, lift_ref,
              out_ref, yf_ref, g_ref, lt_ref):
    recv = [r2lo[...], r2hi[...], r2glo[...], r2ghi[...]]
    out = _finish(bv_ref, yp_ref, recv, fn_ref, _lift_parts(lift_ref, lt_ref), slot_ref, face_ref,
                  g_ref, yf_ref)
    _store_field(out_ref, out)


def _vmem():
    return pl.BlockSpec(memory_space=pltpu.VMEM)


def _smem():
    return pl.BlockSpec(memory_space=pltpu.SMEM)


def _sds(shape):
    return jax.ShapeDtypeStruct(shape, F32)


def exchange(lo, hi, gup, gdn):
    n_dom = lax.axis_size("dom")
    n_grp = lax.axis_size("grp")
    from_lo = lax.ppermute(hi, "dom", [(i, i + 1) for i in range(n_dom - 1)])
    from_hi = lax.ppermute(lo, "dom", [(i + 1, i) for i in range(n_dom - 1)])
    from_glo = lax.ppermute(gup, "grp", [(i, i + 1) for i in range(n_grp - 1)])
    from_ghi = lax.ppermute(gdn, "grp", [(i + 1, i) for i in range(n_grp - 1)])
    return from_lo, from_hi, from_glo, from_ghi


def exchange_fault(lo, hi, g):
    n_dom = lax.axis_size("dom")
    axes = ("grp", "dom")
    from_lo = lax.ppermute(hi, axes, [(i, i + 1) for i in range(n_dom - 1)])
    from_hi = lax.ppermute(lo, axes, [(i + 1, i) for i in range(n_dom - 1)])
    from_ghi = lax.ppermute(g, axes, [(n_dom + i, i) for i in range(n_dom)])
    return from_lo, from_hi, from_ghi


def local(state, star, flux_own, flux_nbr, stiff, trace, lift, nbr_slot, nbr_face, send_slot):
    grp = lax.axis_index("grp").astype(jnp.int32).reshape(1)
    x0 = jnp.transpose(state, (1, 0, 2))
    star = jnp.transpose(star, (1, 2, 0, 3))
    flux_own = jnp.transpose(flux_own, (1, 2, 0, 3))
    flux_nbr = jnp.transpose(flux_nbr, (1, 2, 0, 3))
    trace = jnp.transpose(trace, (1, 0, 2))
    lift = jnp.transpose(lift, (2, 0, 1))
    send = send_slot

    field = _sds((NQ, NB, E))
    flat = _sds((NB, LN))
    table = _sds((TR, 4 * E))
    part = _sds((TR, E))
    yflux = _sds((4 * FP, LN))
    wide = pltpu.VMEM((NB, LN), F32)
    amat = pltpu.VMEM((3 * NB, LN), F32)
    tab = pltpu.VMEM((TR, 4 * E), F32)
    ytr = pltpu.VMEM((NQ, 4 * NF, E), F32)
    yfs = pltpu.VMEM((4 * FP, LN), F32)
    lts = pltpu.VMEM((4 * NF, E), F32)

    first, later, t1, s1lo, s1hi, s1g = pl.pallas_call(
        _kernel_a1,
        out_shape=(flat, flat, table, part, part, part),
        in_specs=[_vmem()] * 5,
        out_specs=tuple([_vmem()] * 6),
        scratch_shapes=[wide, amat, wide, wide, ytr],
    )(x0, star, stiff, trace, send)

    r1 = exchange_fault(s1lo, s1hi, s1g)

    fl, t1l, plo, phi, pg, slg, bv1, yp1 = pl.pallas_call(
        _kernel_a2,
        out_shape=(flat, table, part, part, part, part, flat, yflux),
        in_specs=[_smem()] + [_vmem()] * 15,
        out_specs=tuple([_vmem()] * 8),
        scratch_shapes=[tab, ytr, pltpu.VMEM((TR, E), F32), pltpu.VMEM((TR, E), F32), amat, wide, tab],
    )(grp, x0, first, later, t1, s1lo, s1hi, s1g, star, flux_own, flux_nbr, stiff, trace, send,
      nbr_slot, nbr_face)

    base, integ, own, elo, ehi, egup, egdn = pl.pallas_call(
        _kernel_b,
        out_shape=(flat, flat, table, part, part, part, part),
        in_specs=[_smem()] + [_vmem()] * 21,
        out_specs=tuple([_vmem()] * 7),
        scratch_shapes=[wide, amat, yfs, tab, wide, ytr, lts],
    )(grp, x0, fl, t1l, s1g, plo, phi, pg, slg, bv1, yp1, *r1, nbr_slot, nbr_face, star, flux_nbr,
      stiff, lift, trace, send)

    r2 = exchange(elo, ehi, egup, egdn)

    bv2, yp2 = pl.pallas_call(
        _kernel_b2,
        out_shape=(flat, yflux),
        in_specs=[_vmem()] * 9,
        out_specs=(_vmem(), _vmem()),
        scratch_shapes=[amat, wide, tab],
    )(base, integ, own, star, flux_own, flux_nbr, stiff, nbr_slot, nbr_face)

    out = pl.pallas_call(
        _kernel_c,
        out_shape=field,
        in_specs=[_vmem()] * 10,
        out_specs=_vmem(),
        scratch_shapes=[yfs, tab, lts],
    )(bv2, yp2, *r2, nbr_slot, nbr_face, flux_nbr, lift)
    return jnp.transpose(out, (1, 0, 2))


def solution(mesh):
    in_specs = (
        P(None, None, ("grp", "dom")),
        P(None, None, None, ("grp", "dom")),
        P(None, None, None, ("grp", "dom")),
        P(None, None, None, ("grp", "dom")),
        P(),
        P(),
        P(),
        P(None, ("grp", "dom")),
        P(None, ("grp", "dom")),
        P(("grp", "dom")),
    )
    out_specs = P(None, None, ("grp", "dom"))
    return jax.shard_map(local, mesh=mesh, in_specs=in_specs, out_specs=out_specs, check_vma=False)
```

```python
import math

import jax
import jax.numpy as jnp
from jax import lax
from jax.experimental import pallas as pl
from jax.experimental.pallas import tpu as pltpu
from jax.sharding import PartitionSpec as P

ORDER = 6
NB = 56
NQ = 9
NF = 21
FP = 24
E = 128
LN = NQ * E
TR = NQ * FP

F32 = jnp.float32

W_FIRST = [0.5 ** (k + 1) / math.factorial(k + 1) for k in range(ORDER)]
W_LATER = [(1.0 - 0.5 ** (k + 1)) / math.factorial(k + 1) for k in range(ORDER)]


BF = jnp.bfloat16


def _bdot(a, b):
    return jnp.dot(a, b, preferred_element_type=F32)


def _split2(x):
    hi = x.astype(BF)
    return hi, (x - hi.astype(F32)).astype(BF)


def _dot3(a, b):
    return _bdot(a[0], b[0]) + (_bdot(a[0], b[1]) + _bdot(a[1], b[0]))


def _tdot(a, b):
    return lax.dot_general(a, b, (((0,), (0,)), ((), ())), preferred_element_type=F32)


def _dot3_t(a, b):
    return _tdot(a[0], b[0]) + (_tdot(a[0], b[1]) + _tdot(a[1], b[0]))


def _rows84(ref):
    return jnp.concatenate([ref[r] for r in range(NF)], axis=0)


def _lhs3(a):
    h, l = _split2(jnp.concatenate([a, jnp.zeros((a.shape[0], 8), F32)], axis=1))
    return jnp.concatenate([h, h, l], axis=1)


def _rhs3(x):
    h, l = _split2(jnp.concatenate([x, jnp.zeros((8, x.shape[1]), F32)], axis=0))
    return jnp.concatenate([h, l, h], axis=0)


def _split3(x):
    hi = x.astype(BF)
    r = x - hi.astype(F32)
    mid = r.astype(BF)
    return hi, mid, (r - mid.astype(F32)).astype(BF)


def _sel(p3, onehot):
    return _bdot(p3, jnp.concatenate([onehot, onehot, onehot], axis=0))


def _pad_rows(x, n):
    return jnp.concatenate([x, jnp.zeros((n - x.shape[0], x.shape[1]), x.dtype)], axis=0)


def _lhs3_t(blocks, n):
    out = []
    for b in blocks:
        h, l = _split2(_pad_rows(b, n))
        out += [h, h, l]
    return jnp.concatenate(out, axis=0)


def _rhs3_rows(blocks, n):
    out = []
    for b in blocks:
        h, l = _split2(_pad_rows(b, n))
        out += [h, l, h]
    return jnp.concatenate(out, axis=0)


def _load_field(ref):
    return jnp.concatenate([ref[p] for p in range(NQ)], axis=1)


def _store_field(ref, val):
    for q in range(NQ):
        ref[q] = val[:, q * E:(q + 1) * E]


def _mix_vol(a_ref, star_ref, out_ref, sign):
    for q in range(NQ):
        acc = None
        for p in range(NQ):
            srow = star_ref[p, q]
            for d in range(3):
                t = a_ref[d * NB:(d + 1) * NB, p * E:(p + 1) * E] * srow[d:d + 1, :]
                acc = t if acc is None else acc + t
        out_ref[:, q * E:(q + 1) * E] = acc if sign > 0 else -acc


def _taylor(x, star_ref, stiff_p, d_ref, a_ref, accs):
    for ref, w in accs:
        ref[...] = w[0] * x
    d_ref[...] = x
    for k in range(ORDER - 1):
        a_ref[...] = _bdot(stiff_p, _rhs3(d_ref[...]))
        _mix_vol(a_ref, star_ref, d_ref, -1)
        dn = d_ref[...]
        for ref, w in accs:
            ref[...] = ref[...] + w[k + 1] * dn


def _table(x, trace_p, yt_ref, t_ref):
    yt = _bdot(trace_p, _rhs3(x))
    for p in range(NQ):
        yt_ref[p] = yt[:, p * E:(p + 1) * E]
    t_ref[...] = jnp.zeros(t_ref.shape, F32)
    for f in range(4):
        for p in range(NQ):
            t_ref[p * FP:p * FP + NF, f * E:(f + 1) * E] = yt_ref[p, pl.ds(f, NF, stride=4), :]


def _send(tables, send_ref, outs):
    rows = lax.broadcasted_iota(jnp.int32, (4 * E, 3 * E), 0)
    onehot = jnp.where(rows == send_ref[...].reshape(1, 3 * E), 1.0, 0.0).astype(BF)
    s = _sel(jnp.concatenate(_split3(jnp.concatenate(tables, axis=0)), axis=1), onehot)
    for i, (lo_ref, hi_ref, g_ref) in enumerate(outs):
        blk = s[i * TR:(i + 1) * TR]
        lo_ref[...] = blk[:, 0:E]
        hi_ref[...] = blk[:, E:2 * E]
        g_ref[...] = blk[:, 2 * E:3 * E]


def _gather(comb, slot_ref, face_ref, g_ref, received):
    rows = lax.broadcasted_iota(jnp.int32, (4 * E, E), 0)
    parts = jnp.concatenate(_split3(comb), axis=1)
    for f in range(4):
        v = slot_ref[f:f + 1, :]
        if received:
            s = v - E
            src = jnp.where(v < E, -1, s + jnp.where(s >= 2 * E, 64, 0))
        else:
            src = jnp.where(v < E, face_ref[f:f + 1, :] * E + v, -1)
        onehot = jnp.where(rows == src, 1.0, 0.0).astype(BF)
        g_ref[:, f * E:(f + 1) * E] = _sel(parts, onehot)


def _fmix(pairs, yf_ref, base_ref=None):
    for q in range(NQ):
        accs = [None] * 4
        for p in range(NQ):
            rows = [fl_ref[p, q] for _, fl_ref in pairs]
            for f in range(4):
                t = None
                for (t_ref, _), row in zip(pairs, rows):
                    u = t_ref[p * FP:(p + 1) * FP, f * E:(f + 1) * E] * row[f:f + 1, :]
                    t = u if t is None else t + u
                accs[f] = t if accs[f] is None else accs[f] + t
        for f in range(4):
            acc = accs[f]
            if base_ref is not None:
                acc = base_ref[f * FP:(f + 1) * FP, q * E:(q + 1) * E] + acc
            yf_ref[f * FP:(f + 1) * FP, q * E:(q + 1) * E] = acc


def _lift_parts(lift_ref, lt_ref):
    lt_ref[:, 0:NB] = _rows84(lift_ref)
    return _lhs3_t([lt_ref[pl.ds(f, NF, stride=4), 0:NB] for f in range(4)], 32)


def _vol(b, x, star_ref, stiff_ref, a_ref, v_ref):
    xr = _rhs3(x)
    for d in range(3):
        a_ref[d * NB:(d + 1) * NB, :] = _tdot(_lhs3_t([stiff_ref[d]], 64), xr)
    _mix_vol(a_ref, star_ref, v_ref, 1)
    return b + v_ref[...]


def _partial(b, x, own_ref, star_ref, fo_ref, fn_ref, stiff_ref, slot_ref, face_ref,
             a_ref, v_ref, g_ref, bv_ref, yp_ref):
    bv_ref[...] = _vol(b, x, star_ref, stiff_ref, a_ref, v_ref)
    _gather(own_ref[...], slot_ref, face_ref, g_ref, False)
    _fmix([(own_ref, fo_ref), (g_ref, fn_ref)], yp_ref)


def _finish(bv_ref, yp_ref, recv, fn_ref, lift_p, slot_ref, face_ref, g_ref, yf_ref):
    _gather(jnp.concatenate(recv, axis=1), slot_ref, face_ref, g_ref, True)
    _fmix([(g_ref, fn_ref)], yf_ref, yp_ref)
    ftot = _tdot(lift_p, _rhs3_rows([yf_ref[f * FP:(f + 1) * FP, :] for f in range(4)], 32))
    return bv_ref[...] - ftot


def _kernel_a1(x_ref, star_ref, stiff_ref, trace_ref, send_ref,
               first_ref, later_ref, t1_ref, s1lo, s1hi, s1g,
               d_ref, a_ref, acc1_ref, acc2_ref, yt_ref):
    x = _load_field(x_ref)
    stiff_st = jnp.concatenate([stiff_ref[d] for d in range(3)], axis=0)
    _taylor(x, star_ref, _lhs3(stiff_st), d_ref, a_ref, [(acc1_ref, W_FIRST), (acc2_ref, W_LATER)])
    first = acc1_ref[...]
    first_ref[...] = first
    later_ref[...] = acc2_ref[...]
    _table(first, _lhs3(_rows84(trace_ref)), yt_ref, t1_ref)
    _send([t1_ref[...]], send_ref, [(s1lo, s1hi, s1g)])


def _kernel_a2(grp_ref, x_ref, first_ref, later_ref, t1_ref, s1lo, s1hi, s1g, star_ref, fo_ref, fn_ref,
               stiff_ref, trace_ref, send_ref, slot_ref, face_ref,
               fl_ref, t1l_ref, plo, phi, pg, slg, bv_ref, yp_ref,
               tl_ref, yt_ref, sllo, slhi, a_ref, v_ref, g_ref):
    @pl.when(grp_ref[0] != 0)
    def _():
        later = later_ref[...]
        fl_ref[...] = first_ref[...] + later
        _table(later, _lhs3(_rows84(trace_ref)), yt_ref, tl_ref)
        t1l_ref[...] = t1_ref[...] + tl_ref[...]
        _send([tl_ref[...]], send_ref, [(sllo, slhi, slg)])
        plo[...] = s1lo[...] + sllo[...]
        phi[...] = s1hi[...] + slhi[...]
        pg[...] = s1g[...] + slg[...]

    @pl.when(grp_ref[0] == 0)
    def _():
        _partial(_load_field(x_ref), first_ref[...], t1_ref, star_ref, fo_ref, fn_ref, stiff_ref,
                 slot_ref, face_ref, a_ref, v_ref, g_ref, bv_ref, yp_ref)


def _kernel_b(grp_ref, x_ref, fl_ref, t1l_ref, s1g, plo, phi, pg, slg, bv_ref, yp_ref,
              r1lo, r1hi, r1ghi, slot_ref, face_ref, star_ref, fn_ref,
              stiff_ref, lift_ref, trace_ref, send_ref,
              base_ref, integ_ref, own_ref, elo, ehi, egup, egdn,
              d_ref, a_ref, yf_ref, g_ref, acc_ref, yt_ref, lt_ref):
    grp = grp_ref[0]

    @pl.when(grp == 0)
    def _():
        recv = [r1lo[...], r1hi[...], jnp.zeros((TR, E), F32), r1ghi[...]]
        mid = _finish(bv_ref, yp_ref, recv, fn_ref, _lift_parts(lift_ref, lt_ref), slot_ref, face_ref,
                      g_ref, yf_ref)
        base_ref[...] = mid
        stiff_st = jnp.concatenate([stiff_ref[d] for d in range(3)], axis=0)
        _taylor(mid, star_ref, _lhs3(stiff_st), d_ref, a_ref, [(acc_ref, W_FIRST)])
        second = acc_ref[...]
        integ_ref[...] = second
        _table(second, _lhs3(_rows84(trace_ref)), yt_ref, own_ref)
        _send([own_ref[...]], send_ref, [(elo, ehi, egdn)])
        egup[...] = s1g[...] + egdn[...]

    @pl.when(grp != 0)
    def _():
        base_ref[...] = _load_field(x_ref)
        integ_ref[...] = fl_ref[...]
        own_ref[...] = t1l_ref[...]
        elo[...] = plo[...]
        ehi[...] = phi[...]
        egup[...] = pg[...]

    @pl.when(grp == 1)
    def _():
        egdn[...] = slg[...]

    @pl.when(grp > 1)
    def _():
        egdn[...] = pg[...]


def _kernel_b2(base_ref, integ_ref, own_ref, star_ref, fo_ref, fn_ref, stiff_ref, slot_ref, face_ref,
               bv_ref, yp_ref, a_ref, v_ref, g_ref):
    _partial(base_ref[...], integ_ref[...], own_ref, star_ref, fo_ref, fn_ref, stiff_ref,
             slot_ref, face_ref, a_ref, v_ref, g_ref, bv_ref, yp_ref)


def _kernel_c(bv_ref, yp_ref, r2lo, r2hi, r2glo, r2ghi, slot_ref, face_ref, fn_ref, lift_ref,
              out_ref, yf_ref, g_ref, lt_ref):
    recv = [r2lo[...], r2hi[...], r2glo[...], r2ghi[...]]
    out = _finish(bv_ref, yp_ref, recv, fn_ref, _lift_parts(lift_ref, lt_ref), slot_ref, face_ref,
                  g_ref, yf_ref)
    _store_field(out_ref, out)


def _vmem():
    return pl.BlockSpec(memory_space=pltpu.VMEM)


def _smem():
    return pl.BlockSpec(memory_space=pltpu.SMEM)


def _sds(shape):
    return jax.ShapeDtypeStruct(shape, F32)


def exchange(lo, hi, gup, gdn):
    n_dom = lax.axis_size("dom")
    n_grp = lax.axis_size("grp")
    from_lo = lax.ppermute(hi, "dom", [(i, i + 1) for i in range(n_dom - 1)])
    from_hi = lax.ppermute(lo, "dom", [(i + 1, i) for i in range(n_dom - 1)])
    from_glo = lax.ppermute(gup, "grp", [(i, i + 1) for i in range(n_grp - 1)])
    from_ghi = lax.ppermute(gdn, "grp", [(i + 1, i) for i in range(n_grp - 1)])
    return from_lo, from_hi, from_glo, from_ghi


def exchange_fault(lo, hi, g):
    n_dom = lax.axis_size("dom")
    axes = ("grp", "dom")
    from_lo = lax.ppermute(hi, axes, [(i, i + 1) for i in range(n_dom - 1)])
    from_hi = lax.ppermute(lo, axes, [(i + 1, i) for i in range(n_dom - 1)])
    from_ghi = lax.ppermute(g, axes, [(n_dom + i, i) for i in range(n_dom)])
    return from_lo, from_hi, from_ghi


def local(state, star, flux_own, flux_nbr, stiff, trace, lift, nbr_slot, nbr_face, send_slot):
    grp = lax.axis_index("grp").astype(jnp.int32).reshape(1)
    x0 = jnp.transpose(state, (1, 0, 2))
    star = jnp.transpose(star, (1, 2, 0, 3))
    flux_own = jnp.transpose(flux_own, (1, 2, 0, 3))
    flux_nbr = jnp.transpose(flux_nbr, (1, 2, 0, 3))
    trace = jnp.transpose(trace, (1, 0, 2))
    lift = jnp.transpose(lift, (2, 0, 1))
    send = send_slot

    field = _sds((NQ, NB, E))
    flat = _sds((NB, LN))
    table = _sds((TR, 4 * E))
    part = _sds((TR, E))
    yflux = _sds((4 * FP, LN))
    wide = pltpu.VMEM((NB, LN), F32)
    amat = pltpu.VMEM((3 * NB, LN), F32)
    tab = pltpu.VMEM((TR, 4 * E), F32)
    ytr = pltpu.VMEM((NQ, 4 * NF, E), F32)
    yfs = pltpu.VMEM((4 * FP, LN), F32)
    lts = pltpu.VMEM((4 * NF, E), F32)

    first, later, t1, s1lo, s1hi, s1g = pl.pallas_call(
        _kernel_a1,
        out_shape=(flat, flat, table, part, part, part),
        in_specs=[_vmem()] * 5,
        out_specs=tuple([_vmem()] * 6),
        scratch_shapes=[wide, amat, wide, wide, ytr],
    )(x0, star, stiff, trace, send)

    r1 = exchange_fault(s1lo, s1hi, s1g)

    fl, t1l, plo, phi, pg, slg, bv1, yp1 = pl.pallas_call(
        _kernel_a2,
        out_shape=(flat, table, part, part, part, part, flat, yflux),
        in_specs=[_smem()] + [_vmem()] * 15,
        out_specs=tuple([_vmem()] * 8),
        scratch_shapes=[tab, ytr, pltpu.VMEM((TR, E), F32), pltpu.VMEM((TR, E), F32), amat, wide, tab],
    )(grp, x0, first, later, t1, s1lo, s1hi, s1g, star, flux_own, flux_nbr, stiff, trace, send,
      nbr_slot, nbr_face)

    base, integ, own, elo, ehi, egup, egdn = pl.pallas_call(
        _kernel_b,
        out_shape=(flat, flat, table, part, part, part, part),
        in_specs=[_smem()] + [_vmem()] * 21,
        out_specs=tuple([_vmem()] * 7),
        scratch_shapes=[wide, amat, yfs, tab, wide, ytr, lts],
    )(grp, x0, fl, t1l, s1g, plo, phi, pg, slg, bv1, yp1, *r1, nbr_slot, nbr_face, star, flux_nbr,
      stiff, lift, trace, send)

    r2 = exchange(elo, ehi, egup, egdn)

    bv2, yp2 = pl.pallas_call(
        _kernel_b2,
        out_shape=(flat, yflux),
        in_specs=[_vmem()] * 9,
        out_specs=(_vmem(), _vmem()),
        scratch_shapes=[amat, wide, tab],
    )(base, integ, own, star, flux_own, flux_nbr, stiff, nbr_slot, nbr_face)

    out = pl.pallas_call(
        _kernel_c,
        out_shape=field,
        in_specs=[_vmem()] * 10,
        out_specs=_vmem(),
        scratch_shapes=[yfs, tab, lts],
    )(bv2, yp2, *r2, nbr_slot, nbr_face, flux_nbr, lift)
    return jnp.transpose(out, (1, 0, 2))


def solution(mesh):
    in_specs = (
        P(None, None, ("grp", "dom")),
        P(None, None, None, ("grp", "dom")),
        P(None, None, None, ("grp", "dom")),
        P(None, None, None, ("grp", "dom")),
        P(),
        P(),
        P(),
        P(None, ("grp", "dom")),
        P(None, ("grp", "dom")),
        P(("grp", "dom")),
    )
    out_specs = P(None, None, ("grp", "dom"))
    return jax.shard_map(local, mesh=mesh, in_specs=in_specs, out_specs=out_specs, check_vma=False)
```

```python
import math

import jax
import jax.numpy as jnp
from jax import lax
from jax.experimental import pallas as pl
from jax.experimental.pallas import tpu as pltpu
from jax.sharding import PartitionSpec as P


ORDER = 6
NB = 56
NQ = 9
NF = 21
FP = 24
E = 128
LN = NQ * E
TR = NQ * FP

F32 = jnp.float32

W_FIRST = [0.5 ** (k + 1) / math.factorial(k + 1) for k in range(ORDER)]
W_LATER = [(1.0 - 0.5 ** (k + 1)) / math.factorial(k + 1) for k in range(ORDER)]


BF = jnp.bfloat16


def _bdot(a, b):
    return jnp.dot(a, b, preferred_element_type=F32)


def _split2(x):
    hi = x.astype(BF)
    return hi, (x - hi.astype(F32)).astype(BF)


def _tdot(a, b):
    return lax.dot_general(a, b, (((0,), (0,)), ((), ())), preferred_element_type=F32)


def _rows84(ref):
    return jnp.concatenate([ref[r] for r in range(NF)], axis=0)


def _lhs3(a):
    h, l = _split2(jnp.concatenate([a, jnp.zeros((a.shape[0], 8), F32)], axis=1))
    return jnp.concatenate([h, h, l], axis=1)


def _rhs3(x):
    h, l = _split2(jnp.concatenate([x, jnp.zeros((8, x.shape[1]), F32)], axis=0))
    return jnp.concatenate([h, l, h], axis=0)


def _split3(x):
    hi = x.astype(BF)
    r = x - hi.astype(F32)
    mid = r.astype(BF)
    return hi, mid, (r - mid.astype(F32)).astype(BF)


def _sel(p3, onehot):
    return _bdot(p3, jnp.concatenate([onehot, onehot, onehot], axis=0))


def _pad_rows(x, n):
    return jnp.concatenate([x, jnp.zeros((n - x.shape[0], x.shape[1]), x.dtype)], axis=0)


def _lhs3_t(blocks, n):
    out = []
    for b in blocks:
        h, l = _split2(_pad_rows(b, n))
        out += [h, h, l]
    return jnp.concatenate(out, axis=0)


def _rhs3_rows(blocks, n):
    out = []
    for b in blocks:
        h, l = _split2(_pad_rows(b, n))
        out += [h, l, h]
    return jnp.concatenate(out, axis=0)


def _load_field(ref):
    return jnp.concatenate([ref[p] for p in range(NQ)], axis=1)


def _store_field(ref, val):
    for q in range(NQ):
        ref[q] = val[:, q * E:(q + 1) * E]


def _mix_vol(a_ref, star_ref, out_ref, sign):
    for q in range(NQ):
        acc = None
        for p in range(NQ):
            srow = star_ref[p, q]
            for d in range(3):
                t = a_ref[d * NB:(d + 1) * NB, p * E:(p + 1) * E] * srow[d:d + 1, :]
                acc = t if acc is None else acc + t
        out_ref[:, q * E:(q + 1) * E] = acc if sign > 0 else -acc


def _taylor(x, star_ref, stiff_p, d_ref, a_ref, accs):
    for ref, w in accs:
        ref[...] = w[0] * x
    d_ref[...] = x
    for k in range(ORDER - 1):
        a_ref[...] = _bdot(stiff_p, _rhs3(d_ref[...]))
        _mix_vol(a_ref, star_ref, d_ref, -1)
        dn = d_ref[...]
        for ref, w in accs:
            ref[...] = ref[...] + w[k + 1] * dn


def _table(x, trace_p, yt_ref, t_ref):
    yt = _bdot(trace_p, _rhs3(x))
    for p in range(NQ):
        yt_ref[p] = yt[:, p * E:(p + 1) * E]
    t_ref[...] = jnp.zeros(t_ref.shape, F32)
    for f in range(4):
        for p in range(NQ):
            t_ref[p * FP:p * FP + NF, f * E:(f + 1) * E] = yt_ref[p, pl.ds(f, NF, stride=4), :]


def _send(tables, send_ref, outs):
    rows = lax.broadcasted_iota(jnp.int32, (4 * E, 3 * E), 0)
    onehot = jnp.where(rows == send_ref[...].reshape(1, 3 * E), 1.0, 0.0).astype(BF)
    s = _sel(jnp.concatenate(_split3(jnp.concatenate(tables, axis=0)), axis=1), onehot)
    for i, (lo_ref, hi_ref, g_ref) in enumerate(outs):
        blk = s[i * TR:(i + 1) * TR]
        lo_ref[...] = blk[:, 0:E]
        hi_ref[...] = blk[:, E:2 * E]
        g_ref[...] = blk[:, 2 * E:3 * E]


def _gather(comb, slot_ref, face_ref, g_ref, received):
    rows = lax.broadcasted_iota(jnp.int32, (4 * E, E), 0)
    parts = jnp.concatenate(_split3(comb), axis=1)
    for f in range(4):
        v = slot_ref[f:f + 1, :]
        if received:
            s = v - E
            src = jnp.where(v < E, -1, s + jnp.where(s >= 2 * E, 64, 0))
        else:
            src = jnp.where(v < E, face_ref[f:f + 1, :] * E + v, -1)
        onehot = jnp.where(rows == src, 1.0, 0.0).astype(BF)
        g_ref[:, f * E:(f + 1) * E] = _sel(parts, onehot)


def _fmix(pairs, yf_ref, base_ref=None):
    for q in range(NQ):
        accs = [None] * 4
        for p in range(NQ):
            rows = [fl_ref[p, q] for _, fl_ref in pairs]
            for f in range(4):
                t = None
                for (t_ref, _), row in zip(pairs, rows):
                    u = t_ref[p * FP:(p + 1) * FP, f * E:(f + 1) * E] * row[f:f + 1, :]
                    t = u if t is None else t + u
                accs[f] = t if accs[f] is None else accs[f] + t
        for f in range(4):
            acc = accs[f]
            if base_ref is not None:
                acc = base_ref[f * FP:(f + 1) * FP, q * E:(q + 1) * E] + acc
            yf_ref[f * FP:(f + 1) * FP, q * E:(q + 1) * E] = acc


def _lift_parts(lift_ref, lt_ref):
    lt_ref[:, 0:NB] = _rows84(lift_ref)
    return _lhs3_t([lt_ref[pl.ds(f, NF, stride=4), 0:NB] for f in range(4)], 32)


def _vol(b, x, star_ref, stiff_ref, a_ref, v_ref):
    xr = _rhs3(x)
    for d in range(3):
        a_ref[d * NB:(d + 1) * NB, :] = _tdot(_lhs3_t([stiff_ref[d]], 64), xr)
    _mix_vol(a_ref, star_ref, v_ref, 1)
    return b + v_ref[...]


def _partial(b, x, own_ref, star_ref, fo_ref, fn_ref, stiff_ref, slot_ref, face_ref,
             a_ref, v_ref, g_ref, bv_ref, yp_ref):
    bv_ref[...] = _vol(b, x, star_ref, stiff_ref, a_ref, v_ref)
    _gather(own_ref[...], slot_ref, face_ref, g_ref, False)
    _fmix([(own_ref, fo_ref), (g_ref, fn_ref)], yp_ref)


def _finish(bv_ref, yp_ref, recv, fn_ref, lift_p, slot_ref, face_ref, g_ref, yf_ref):
    _gather(jnp.concatenate(recv, axis=1), slot_ref, face_ref, g_ref, True)
    _fmix([(g_ref, fn_ref)], yf_ref, yp_ref)
    ftot = _tdot(lift_p, _rhs3_rows([yf_ref[f * FP:(f + 1) * FP, :] for f in range(4)], 32))
    return bv_ref[...] - ftot


def _kernel_a1(x_ref, star_ref, stiff_ref, trace_ref, send_ref,
               first_ref, later_ref, t1_ref, s1lo, s1hi, s1g,
               d_ref, a_ref, acc1_ref, acc2_ref, yt_ref):
    x = _load_field(x_ref)
    stiff_st = jnp.concatenate([stiff_ref[d] for d in range(3)], axis=0)
    _taylor(x, star_ref, _lhs3(stiff_st), d_ref, a_ref, [(acc1_ref, W_FIRST), (acc2_ref, W_LATER)])
    first = acc1_ref[...]
    first_ref[...] = first
    later_ref[...] = acc2_ref[...]
    _table(first, _lhs3(_rows84(trace_ref)), yt_ref, t1_ref)
    _send([t1_ref[...]], send_ref, [(s1lo, s1hi, s1g)])


def _kernel_a2(grp_ref, x_ref, first_ref, later_ref, t1_ref, s1lo, s1hi, s1g, star_ref, fo_ref, fn_ref,
               stiff_ref, trace_ref, send_ref, slot_ref, face_ref,
               fl_ref, t1l_ref, plo, phi, pg, slg, bv_ref, yp_ref,
               tl_ref, yt_ref, sllo, slhi, a_ref, v_ref, g_ref):
    @pl.when(grp_ref[0] != 0)
    def _():
        later = later_ref[...]
        fl_ref[...] = first_ref[...] + later
        _table(later, _lhs3(_rows84(trace_ref)), yt_ref, tl_ref)
        t1l_ref[...] = t1_ref[...] + tl_ref[...]
        _send([tl_ref[...]], send_ref, [(sllo, slhi, slg)])
        plo[...] = s1lo[...] + sllo[...]
        phi[...] = s1hi[...] + slhi[...]
        pg[...] = s1g[...] + slg[...]

    @pl.when(grp_ref[0] == 0)
    def _():
        _partial(_load_field(x_ref), first_ref[...], t1_ref, star_ref, fo_ref, fn_ref, stiff_ref,
                 slot_ref, face_ref, a_ref, v_ref, g_ref, bv_ref, yp_ref)


def _kernel_b(grp_ref, x_ref, fl_ref, t1l_ref, s1g, plo, phi, pg, slg, bv_ref, yp_ref,
              r1lo, r1hi, r1ghi, slot_ref, face_ref, star_ref, fn_ref,
              stiff_ref, lift_ref, trace_ref, send_ref,
              base_ref, integ_ref, own_ref, elo, ehi, egup, egdn,
              d_ref, a_ref, yf_ref, g_ref, acc_ref, yt_ref, lt_ref):
    grp = grp_ref[0]

    @pl.when(grp == 0)
    def _():
        recv = [r1lo[...], r1hi[...], jnp.zeros((TR, E), F32), r1ghi[...]]
        mid = _finish(bv_ref, yp_ref, recv, fn_ref, _lift_parts(lift_ref, lt_ref), slot_ref, face_ref,
                      g_ref, yf_ref)
        base_ref[...] = mid
        stiff_st = jnp.concatenate([stiff_ref[d] for d in range(3)], axis=0)
        _taylor(mid, star_ref, _lhs3(stiff_st), d_ref, a_ref, [(acc_ref, W_FIRST)])
        second = acc_ref[...]
        integ_ref[...] = second
        _table(second, _lhs3(_rows84(trace_ref)), yt_ref, own_ref)
        _send([own_ref[...]], send_ref, [(elo, ehi, egdn)])
        egup[...] = s1g[...] + egdn[...]

    @pl.when(grp != 0)
    def _():
        base_ref[...] = _load_field(x_ref)
        integ_ref[...] = fl_ref[...]
        own_ref[...] = t1l_ref[...]
        elo[...] = plo[...]
        ehi[...] = phi[...]
        egup[...] = pg[...]

    @pl.when(grp == 1)
    def _():
        egdn[...] = slg[...]

    @pl.when(grp > 1)
    def _():
        egdn[...] = pg[...]


def _kernel_b2(base_ref, integ_ref, own_ref, star_ref, fo_ref, fn_ref, stiff_ref, slot_ref, face_ref,
               bv_ref, yp_ref, a_ref, v_ref, g_ref):
    _partial(base_ref[...], integ_ref[...], own_ref, star_ref, fo_ref, fn_ref, stiff_ref,
             slot_ref, face_ref, a_ref, v_ref, g_ref, bv_ref, yp_ref)


def _kernel_c(bv_ref, yp_ref, r2lo, r2hi, r2glo, r2ghi, slot_ref, face_ref, fn_ref, lift_ref,
              out_ref, yf_ref, g_ref, lt_ref):
    recv = [r2lo[...], r2hi[...], r2glo[...], r2ghi[...]]
    out = _finish(bv_ref, yp_ref, recv, fn_ref, _lift_parts(lift_ref, lt_ref), slot_ref, face_ref,
                  g_ref, yf_ref)
    _store_field(out_ref, out)


def _vmem():
    return pl.BlockSpec(memory_space=pltpu.VMEM)


def _smem():
    return pl.BlockSpec(memory_space=pltpu.SMEM)


def _sds(shape):
    return jax.ShapeDtypeStruct(shape, F32)


def exchange(lo, hi, gup, gdn):
    n_dom = lax.axis_size("dom")
    n_grp = lax.axis_size("grp")
    from_ghi = lax.ppermute(gdn, "grp", [(i + 1, i) for i in range(n_grp - 1)])
    from_glo = lax.ppermute(gup, "grp", [(i, i + 1) for i in range(n_grp - 1)])
    from_lo = lax.ppermute(hi, "dom", [(i, i + 1) for i in range(n_dom - 1)])
    from_hi = lax.ppermute(lo, "dom", [(i + 1, i) for i in range(n_dom - 1)])
    return from_lo, from_hi, from_glo, from_ghi


def exchange_fault(lo, hi, g):
    n_dom = lax.axis_size("dom")
    axes = ("grp", "dom")
    from_ghi = lax.ppermute(g, axes, [(n_dom + i, i) for i in range(n_dom)])
    from_lo = lax.ppermute(hi, axes, [(i, i + 1) for i in range(n_dom - 1)])
    from_hi = lax.ppermute(lo, axes, [(i + 1, i) for i in range(n_dom - 1)])
    return from_lo, from_hi, from_ghi


def _local(state, star, flux_own, flux_nbr, stiff, trace, lift, nbr_slot, nbr_face, send_slot):
    grp = lax.axis_index("grp").astype(jnp.int32).reshape(1)
    x0 = jnp.transpose(state, (1, 0, 2))
    star = jnp.transpose(star, (1, 2, 0, 3))
    flux_own = jnp.transpose(flux_own, (1, 2, 0, 3))
    flux_nbr = jnp.transpose(flux_nbr, (1, 2, 0, 3))
    trace = jnp.transpose(trace, (1, 0, 2))
    lift = jnp.transpose(lift, (2, 0, 1))
    send = send_slot

    field = _sds((NQ, NB, E))
    flat = _sds((NB, LN))
    table = _sds((TR, 4 * E))
    part = _sds((TR, E))
    yflux = _sds((4 * FP, LN))
    wide = pltpu.VMEM((NB, LN), F32)
    amat = pltpu.VMEM((3 * NB, LN), F32)
    tab = pltpu.VMEM((TR, 4 * E), F32)
    ytr = pltpu.VMEM((NQ, 4 * NF, E), F32)
    yfs = pltpu.VMEM((4 * FP, LN), F32)
    lts = pltpu.VMEM((4 * NF, E), F32)

    first, later, t1, s1lo, s1hi, s1g = pl.pallas_call(
        _kernel_a1,
        out_shape=(flat, flat, table, part, part, part),
        in_specs=[_vmem()] * 5,
        out_specs=tuple([_vmem()] * 6),
        scratch_shapes=[wide, amat, wide, wide, ytr],
    )(x0, star, stiff, trace, send)

    r1 = exchange_fault(s1lo, s1hi, s1g)

    fl, t1l, plo, phi, pg, slg, bv1, yp1 = pl.pallas_call(
        _kernel_a2,
        out_shape=(flat, table, part, part, part, part, flat, yflux),
        in_specs=[_smem()] + [_vmem()] * 15,
        out_specs=tuple([_vmem()] * 8),
        scratch_shapes=[tab, ytr, pltpu.VMEM((TR, E), F32), pltpu.VMEM((TR, E), F32), amat, wide, tab],
    )(grp, x0, first, later, t1, s1lo, s1hi, s1g, star, flux_own, flux_nbr, stiff, trace, send,
      nbr_slot, nbr_face)

    base, integ, own, elo, ehi, egup, egdn = pl.pallas_call(
        _kernel_b,
        out_shape=(flat, flat, table, part, part, part, part),
        in_specs=[_smem()] + [_vmem()] * 21,
        out_specs=tuple([_vmem()] * 7),
        scratch_shapes=[wide, amat, yfs, tab, wide, ytr, lts],
    )(grp, x0, fl, t1l, s1g, plo, phi, pg, slg, bv1, yp1, *r1, nbr_slot, nbr_face, star, flux_nbr,
      stiff, lift, trace, send)

    r2 = exchange(elo, ehi, egup, egdn)

    bv2, yp2 = pl.pallas_call(
        _kernel_b2,
        out_shape=(flat, yflux),
        in_specs=[_vmem()] * 9,
        out_specs=(_vmem(), _vmem()),
        scratch_shapes=[amat, wide, tab],
    )(base, integ, own, star, flux_own, flux_nbr, stiff, nbr_slot, nbr_face)

    out = pl.pallas_call(
        _kernel_c,
        out_shape=field,
        in_specs=[_vmem()] * 10,
        out_specs=_vmem(),
        scratch_shapes=[yfs, tab, lts],
    )(bv2, yp2, *r2, nbr_slot, nbr_face, flux_nbr, lift)
    return jnp.transpose(out, (1, 0, 2))


def solution(mesh):
    in_specs = (
        P(None, None, ("grp", "dom")),
        P(None, None, None, ("grp", "dom")),
        P(None, None, None, ("grp", "dom")),
        P(None, None, None, ("grp", "dom")),
        P(),
        P(),
        P(),
        P(None, ("grp", "dom")),
        P(None, ("grp", "dom")),
        P(("grp", "dom")),
    )
    out_specs = P(None, None, ("grp", "dom"))
    return jax.shard_map(_local, mesh=mesh, in_specs=in_specs, out_specs=out_specs, check_vma=False)
```

```python
import math

import jax
import jax.numpy as jnp
from jax import lax
from jax.experimental import pallas as pl
from jax.experimental.pallas import tpu as pltpu
from jax.sharding import PartitionSpec as P

ORDER = 6
NB = 56
NQ = 9
NF = 21
FP = 24
E = 128
LN = NQ * E
TR = NQ * FP

F32 = jnp.float32

W_FIRST = [0.5 ** (k + 1) / math.factorial(k + 1) for k in range(ORDER)]
W_LATER = [(1.0 - 0.5 ** (k + 1)) / math.factorial(k + 1) for k in range(ORDER)]
W_FIRST = [w * (-1) ** k for k, w in enumerate(W_FIRST)]
W_LATER = [w * (-1) ** k for k, w in enumerate(W_LATER)]


BF = jnp.bfloat16


def _bdot(a, b):
    return jnp.dot(a, b, preferred_element_type=F32)


def _split2(x):
    hi = x.astype(BF)
    return hi, (x - hi.astype(F32)).astype(BF)


def _dot3(a, b):
    return _bdot(a[0], b[0]) + (_bdot(a[0], b[1]) + _bdot(a[1], b[0]))


def _tdot(a, b):
    return lax.dot_general(a, b, (((0,), (0,)), ((), ())), preferred_element_type=F32)


def _dot3_t(a, b):
    return _tdot(a[0], b[0]) + (_tdot(a[0], b[1]) + _tdot(a[1], b[0]))


def _rows84(ref):
    return jnp.concatenate([ref[r] for r in range(NF)], axis=0)


def _lhs3(a):
    h, l = _split2(jnp.concatenate([a, jnp.zeros((a.shape[0], 8), F32)], axis=1))
    return jnp.concatenate([h, h, l], axis=1)


def _rhs3(x):
    h, l = _split2(jnp.concatenate([x, jnp.zeros((8, x.shape[1]), F32)], axis=0))
    return jnp.concatenate([h, l, h], axis=0)


def _split3(x):
    hi = x.astype(BF)
    r = x - hi.astype(F32)
    mid = r.astype(BF)
    return hi, mid, (r - mid.astype(F32)).astype(BF)


def _sel(p3, onehot):
    return _bdot(p3, jnp.concatenate([onehot, onehot, onehot], axis=0))


def _pad_rows(x, n):
    return jnp.concatenate([x, jnp.zeros((n - x.shape[0], x.shape[1]), x.dtype)], axis=0)


def _lhs3_t(blocks, n):
    out = []
    for b in blocks:
        h, l = _split2(_pad_rows(b, n))
        out += [h, h, l]
    return jnp.concatenate(out, axis=0)


def _rhs3_rows(blocks, n):
    out = []
    for b in blocks:
        h, l = _split2(_pad_rows(b, n))
        out += [h, l, h]
    return jnp.concatenate(out, axis=0)


def _load_field(ref):
    return jnp.concatenate([ref[p] for p in range(NQ)], axis=1)


def _store_field(ref, val):
    for q in range(NQ):
        ref[q] = val[:, q * E:(q + 1) * E]


def _mix_vol(a_ref, star_ref, out_ref, sign):
    for q in range(NQ):
        acc = None
        for p in range(NQ):
            srow = star_ref[p, q]
            for d in range(3):
                t = a_ref[d * NB:(d + 1) * NB, p * E:(p + 1) * E] * srow[d:d + 1, :]
                acc = t if acc is None else acc + t
        out_ref[:, q * E:(q + 1) * E] = acc if sign > 0 else -acc


def _taylor(x, star_ref, stiff_p, d_ref, a_ref, accs):
    for ref, w in accs:
        ref[...] = w[0] * x
    d_ref[...] = x
    for k in range(ORDER - 1):
        a_ref[...] = _bdot(stiff_p, _rhs3(d_ref[...]))
        _mix_vol(a_ref, star_ref, d_ref, 1)
        dn = d_ref[...]
        for ref, w in accs:
            ref[...] = ref[...] + w[k + 1] * dn


def _table(x, trace_p, yt_ref, t_ref):
    yt = _bdot(trace_p, _rhs3(x))
    for p in range(NQ):
        yt_ref[p] = yt[:, p * E:(p + 1) * E]
    t_ref[...] = jnp.zeros(t_ref.shape, F32)
    for f in range(4):
        for p in range(NQ):
            t_ref[p * FP:p * FP + NF, f * E:(f + 1) * E] = yt_ref[p, pl.ds(f, NF, stride=4), :]


def _send(tables, send_ref, outs):
    rows = lax.broadcasted_iota(jnp.int32, (4 * E, 3 * E), 0)
    onehot = jnp.where(rows == send_ref[...].reshape(1, 3 * E), 1.0, 0.0).astype(BF)
    s = _sel(jnp.concatenate(_split3(jnp.concatenate(tables, axis=0)), axis=1), onehot)
    for i, (lo_ref, hi_ref, g_ref) in enumerate(outs):
        blk = s[i * TR:(i + 1) * TR]
        lo_ref[...] = blk[:, 0:E]
        hi_ref[...] = blk[:, E:2 * E]
        g_ref[...] = blk[:, 2 * E:3 * E]


def _gather(comb, slot_ref, face_ref, g_ref, received):
    rows = lax.broadcasted_iota(jnp.int32, (4 * E, E), 0)
    parts = jnp.concatenate(_split3(comb), axis=1)
    for f in range(4):
        v = slot_ref[f:f + 1, :]
        if received:
            s = v - E
            src = jnp.where(v < E, -1, s + jnp.where(s >= 2 * E, 64, 0))
        else:
            src = jnp.where(v < E, face_ref[f:f + 1, :] * E + v, -1)
        onehot = jnp.where(rows == src, 1.0, 0.0).astype(BF)
        g_ref[:, f * E:(f + 1) * E] = _sel(parts, onehot)


def _fmix(pairs, yf_ref, base_ref=None):
    for q in range(NQ):
        accs = [None] * 4
        for p in range(NQ):
            rows = [fl_ref[p, q] for _, fl_ref in pairs]
            for f in range(4):
                t = None
                for (t_ref, _), row in zip(pairs, rows):
                    u = t_ref[p * FP:(p + 1) * FP, f * E:(f + 1) * E] * row[f:f + 1, :]
                    t = u if t is None else t + u
                accs[f] = t if accs[f] is None else accs[f] + t
        for f in range(4):
            acc = accs[f]
            if base_ref is not None:
                acc = base_ref[f * FP:(f + 1) * FP, q * E:(q + 1) * E] + acc
            yf_ref[f * FP:(f + 1) * FP, q * E:(q + 1) * E] = acc


def _lift_parts(lift_ref, lt_ref):
    lt_ref[:, 0:NB] = _rows84(lift_ref)
    return _lhs3_t([lt_ref[pl.ds(f, NF, stride=4), 0:NB] for f in range(4)], 32)


def _vol(b, x, star_ref, stiff_ref, a_ref, v_ref):
    xr = _rhs3(x)
    for d in range(3):
        a_ref[d * NB:(d + 1) * NB, :] = _tdot(_lhs3_t([stiff_ref[d]], 64), xr)
    _mix_vol(a_ref, star_ref, v_ref, 1)
    return b + v_ref[...]


def _partial(b, x, own_ref, star_ref, fo_ref, fn_ref, stiff_ref, slot_ref, face_ref,
             a_ref, v_ref, g_ref, bv_ref, yp_ref):
    bv_ref[...] = _vol(b, x, star_ref, stiff_ref, a_ref, v_ref)
    _gather(own_ref[...], slot_ref, face_ref, g_ref, False)
    _fmix([(own_ref, fo_ref), (g_ref, fn_ref)], yp_ref)


def _finish(bv_ref, yp_ref, recv, fn_ref, lift_p, slot_ref, face_ref, g_ref, yf_ref):
    _gather(jnp.concatenate(recv, axis=1), slot_ref, face_ref, g_ref, True)
    _fmix([(g_ref, fn_ref)], yf_ref, yp_ref)
    ftot = _tdot(lift_p, _rhs3_rows([yf_ref[f * FP:(f + 1) * FP, :] for f in range(4)], 32))
    return bv_ref[...] - ftot


def _kernel_a1(grp_ref, x_ref, star_ref, stiff_ref, trace_ref, send_ref,
               first_ref, later_ref, t1_ref, s1lo, s1hi, s1g,
               d_ref, a_ref, acc1_ref, acc2_ref, yt_ref):
    x = _load_field(x_ref)
    stiff_p = _lhs3(jnp.concatenate([stiff_ref[d] for d in range(3)], axis=0))

    @pl.when(grp_ref[0] == 0)
    def _():
        _taylor(x, star_ref, stiff_p, d_ref, a_ref, [(acc1_ref, W_FIRST)])

    @pl.when(grp_ref[0] != 0)
    def _():
        _taylor(x, star_ref, stiff_p, d_ref, a_ref, [(acc1_ref, W_FIRST), (acc2_ref, W_LATER)])
        later_ref[...] = acc2_ref[...]

    first = acc1_ref[...]
    first_ref[...] = first
    _table(first, _lhs3(_rows84(trace_ref)), yt_ref, t1_ref)
    _send([t1_ref[...]], send_ref, [(s1lo, s1hi, s1g)])


def _kernel_a2(grp_ref, x_ref, first_ref, later_ref, t1_ref, s1lo, s1hi, s1g, star_ref, fo_ref, fn_ref,
               stiff_ref, trace_ref, send_ref, slot_ref, face_ref,
               fl_ref, t1l_ref, plo, phi, pg, slg, bv_ref, yp_ref,
               tl_ref, yt_ref, sllo, slhi, a_ref, v_ref, g_ref):
    @pl.when(grp_ref[0] != 0)
    def _():
        later = later_ref[...]
        fl_ref[...] = first_ref[...] + later
        _table(later, _lhs3(_rows84(trace_ref)), yt_ref, tl_ref)
        t1l_ref[...] = t1_ref[...] + tl_ref[...]
        _send([tl_ref[...]], send_ref, [(sllo, slhi, slg)])
        plo[...] = s1lo[...] + sllo[...]
        phi[...] = s1hi[...] + slhi[...]
        pg[...] = s1g[...] + slg[...]

    @pl.when(grp_ref[0] == 0)
    def _():
        _partial(_load_field(x_ref), first_ref[...], t1_ref, star_ref, fo_ref, fn_ref, stiff_ref,
                 slot_ref, face_ref, a_ref, v_ref, g_ref, bv_ref, yp_ref)


def _kernel_b(grp_ref, x_ref, fl_ref, t1l_ref, s1g, plo, phi, pg, slg, bv_ref, yp_ref,
              r1lo, r1hi, r1ghi, slot_ref, face_ref, star_ref, fn_ref,
              stiff_ref, lift_ref, trace_ref, send_ref,
              base_ref, integ_ref, own_ref, elo, ehi, egup, egdn,
              d_ref, a_ref, yf_ref, g_ref, acc_ref, yt_ref, lt_ref):
    grp = grp_ref[0]

    @pl.when(grp == 0)
    def _():
        recv = [r1lo[...], r1hi[...], jnp.zeros((TR, E), F32), r1ghi[...]]
        mid = _finish(bv_ref, yp_ref, recv, fn_ref, _lift_parts(lift_ref, lt_ref), slot_ref, face_ref,
                      g_ref, yf_ref)
        base_ref[...] = mid
        stiff_st = jnp.concatenate([stiff_ref[d] for d in range(3)], axis=0)
        _taylor(mid, star_ref, _lhs3(stiff_st), d_ref, a_ref, [(acc_ref, W_FIRST)])
        second = acc_ref[...]
        integ_ref[...] = second
        _table(second, _lhs3(_rows84(trace_ref)), yt_ref, own_ref)
        _send([own_ref[...]], send_ref, [(elo, ehi, egdn)])
        egup[...] = s1g[...] + egdn[...]

    @pl.when(grp != 0)
    def _():
        base_ref[...] = _load_field(x_ref)
        integ_ref[...] = fl_ref[...]
        own_ref[...] = t1l_ref[...]
        elo[...] = plo[...]
        ehi[...] = phi[...]
        egup[...] = pg[...]

    @pl.when(grp == 1)
    def _():
        egdn[...] = slg[...]

    @pl.when(grp > 1)
    def _():
        egdn[...] = pg[...]


def _kernel_b2(base_ref, integ_ref, own_ref, star_ref, fo_ref, fn_ref, stiff_ref, slot_ref, face_ref,
               bv_ref, yp_ref, a_ref, v_ref, g_ref):
    _partial(base_ref[...], integ_ref[...], own_ref, star_ref, fo_ref, fn_ref, stiff_ref,
             slot_ref, face_ref, a_ref, v_ref, g_ref, bv_ref, yp_ref)


def _kernel_c(bv_ref, yp_ref, r2lo, r2hi, r2glo, r2ghi, slot_ref, face_ref, fn_ref, lift_ref,
              out_ref, yf_ref, g_ref, lt_ref):
    recv = [r2lo[...], r2hi[...], r2glo[...], r2ghi[...]]
    out = _finish(bv_ref, yp_ref, recv, fn_ref, _lift_parts(lift_ref, lt_ref), slot_ref, face_ref,
                  g_ref, yf_ref)
    _store_field(out_ref, out)


def _vmem():
    return pl.BlockSpec(memory_space=pltpu.VMEM)


def _smem():
    return pl.BlockSpec(memory_space=pltpu.SMEM)


def _sds(shape):
    return jax.ShapeDtypeStruct(shape, F32)


def exchange(lo, hi, gup, gdn):
    n_dom = lax.axis_size("dom")
    n_grp = lax.axis_size("grp")
    from_lo = lax.ppermute(hi, "dom", [(i, i + 1) for i in range(n_dom - 1)])
    from_hi = lax.ppermute(lo, "dom", [(i + 1, i) for i in range(n_dom - 1)])
    from_glo = lax.ppermute(gup, "grp", [(i, i + 1) for i in range(n_grp - 1)])
    from_ghi = lax.ppermute(gdn, "grp", [(i + 1, i) for i in range(n_grp - 1)])
    return from_lo, from_hi, from_glo, from_ghi


def exchange_fault(lo, hi, g):
    n_dom = lax.axis_size("dom")
    axes = ("grp", "dom")
    from_lo = lax.ppermute(hi, axes, [(i, i + 1) for i in range(n_dom - 1)])
    from_hi = lax.ppermute(lo, axes, [(i + 1, i) for i in range(n_dom - 1)])
    from_ghi = lax.ppermute(g, axes, [(n_dom + i, i) for i in range(n_dom)])
    return from_lo, from_hi, from_ghi


def local(state, star, flux_own, flux_nbr, stiff, trace, lift, nbr_slot, nbr_face, send_slot):
    grp = lax.axis_index("grp").astype(jnp.int32).reshape(1)
    x0 = jnp.transpose(state, (1, 0, 2))
    star = jnp.transpose(star, (1, 2, 0, 3))
    flux_own = jnp.transpose(flux_own, (1, 2, 0, 3))
    flux_nbr = jnp.transpose(flux_nbr, (1, 2, 0, 3))
    trace = jnp.transpose(trace, (1, 0, 2))
    lift = jnp.transpose(lift, (2, 0, 1))
    send = send_slot

    field = _sds((NQ, NB, E))
    flat = _sds((NB, LN))
    table = _sds((TR, 4 * E))
    part = _sds((TR, E))
    yflux = _sds((4 * FP, LN))
    wide = pltpu.VMEM((NB, LN), F32)
    amat = pltpu.VMEM((3 * NB, LN), F32)
    tab = pltpu.VMEM((TR, 4 * E), F32)
    ytr = pltpu.VMEM((NQ, 4 * NF, E), F32)
    yfs = pltpu.VMEM((4 * FP, LN), F32)
    lts = pltpu.VMEM((4 * NF, E), F32)

    first, later, t1, s1lo, s1hi, s1g = pl.pallas_call(
        _kernel_a1,
        out_shape=(flat, flat, table, part, part, part),
        in_specs=[_smem()] + [_vmem()] * 5,
        out_specs=tuple([_vmem()] * 6),
        scratch_shapes=[wide, amat, wide, wide, ytr],
    )(grp, x0, star, stiff, trace, send)

    r1 = exchange_fault(s1lo, s1hi, s1g)

    fl, t1l, plo, phi, pg, slg, bv1, yp1 = pl.pallas_call(
        _kernel_a2,
        out_shape=(flat, table, part, part, part, part, flat, yflux),
        in_specs=[_smem()] + [_vmem()] * 15,
        out_specs=tuple([_vmem()] * 8),
        scratch_shapes=[tab, ytr, pltpu.VMEM((TR, E), F32), pltpu.VMEM((TR, E), F32), amat, wide, tab],
    )(grp, x0, first, later, t1, s1lo, s1hi, s1g, star, flux_own, flux_nbr, stiff, trace, send,
      nbr_slot, nbr_face)

    base, integ, own, elo, ehi, egup, egdn = pl.pallas_call(
        _kernel_b,
        out_shape=(flat, flat, table, part, part, part, part),
        in_specs=[_smem()] + [_vmem()] * 21,
        out_specs=tuple([_vmem()] * 7),
        scratch_shapes=[wide, amat, yfs, tab, wide, ytr, lts],
    )(grp, x0, fl, t1l, s1g, plo, phi, pg, slg, bv1, yp1, *r1, nbr_slot, nbr_face, star, flux_nbr,
      stiff, lift, trace, send)

    r2 = exchange(elo, ehi, egup, egdn)

    bv2, yp2 = pl.pallas_call(
        _kernel_b2,
        out_shape=(flat, yflux),
        in_specs=[_vmem()] * 9,
        out_specs=(_vmem(), _vmem()),
        scratch_shapes=[amat, wide, tab],
    )(base, integ, own, star, flux_own, flux_nbr, stiff, nbr_slot, nbr_face)

    out = pl.pallas_call(
        _kernel_c,
        out_shape=field,
        in_specs=[_vmem()] * 10,
        out_specs=_vmem(),
        scratch_shapes=[yfs, tab, lts],
    )(bv2, yp2, *r2, nbr_slot, nbr_face, flux_nbr, lift)
    return jnp.transpose(out, (1, 0, 2))


def solution(mesh):
    in_specs = (
        P(None, None, ("grp", "dom")),
        P(None, None, None, ("grp", "dom")),
        P(None, None, None, ("grp", "dom")),
        P(None, None, None, ("grp", "dom")),
        P(),
        P(),
        P(),
        P(None, ("grp", "dom")),
        P(None, ("grp", "dom")),
        P(("grp", "dom")),
    )
    out_specs = P(None, None, ("grp", "dom"))
    return jax.shard_map(local, mesh=mesh, in_specs=in_specs, out_specs=out_specs, check_vma=False)
```

```python
import math

import jax
import jax.numpy as jnp
from jax import lax
from jax.experimental import pallas as pl
from jax.experimental.pallas import tpu as pltpu
from jax.sharding import PartitionSpec as P

ORDER = 6
NB = 56
NQ = 9
NF = 21
FP = 24
E = 128
LN = NQ * E
TR = NQ * FP

F32 = jnp.float32

W_FIRST = [0.5 ** (k + 1) / math.factorial(k + 1) for k in range(ORDER)]
W_LATER = [(1.0 - 0.5 ** (k + 1)) / math.factorial(k + 1) for k in range(ORDER)]


BF = jnp.bfloat16


def _bdot(a, b):
    return jnp.dot(a, b, preferred_element_type=F32)


def _split2(x):
    hi = x.astype(BF)
    return hi, (x - hi.astype(F32)).astype(BF)


def _dot3(a, b):
    return _bdot(a[0], b[0]) + (_bdot(a[0], b[1]) + _bdot(a[1], b[0]))


def _tdot(a, b):
    return lax.dot_general(a, b, (((0,), (0,)), ((), ())), preferred_element_type=F32)


def _dot3_t(a, b):
    return _tdot(a[0], b[0]) + (_tdot(a[0], b[1]) + _tdot(a[1], b[0]))


def _rows84(ref):
    return jnp.concatenate([ref[r] for r in range(NF)], axis=0)


def _lhs3(a):
    h, l = _split2(jnp.concatenate([a, jnp.zeros((a.shape[0], 8), F32)], axis=1))
    return jnp.concatenate([h, h, l], axis=1)


def _rhs3(x):
    h, l = _split2(jnp.concatenate([x, jnp.zeros((8, x.shape[1]), F32)], axis=0))
    return jnp.concatenate([h, l, h], axis=0)


def _split3(x):
    hi = x.astype(BF)
    r = x - hi.astype(F32)
    mid = r.astype(BF)
    return hi, mid, (r - mid.astype(F32)).astype(BF)


def _sel(p3, onehot):
    return _bdot(p3, jnp.concatenate([onehot, onehot, onehot], axis=0))


def _pad_rows(x, n):
    return jnp.concatenate([x, jnp.zeros((n - x.shape[0], x.shape[1]), x.dtype)], axis=0)


def _lhs3_t(blocks, n):
    out = []
    for b in blocks:
        h, l = _split2(_pad_rows(b, n))
        out += [h, h, l]
    return jnp.concatenate(out, axis=0)


def _rhs3_rows(blocks, n):
    out = []
    for b in blocks:
        h, l = _split2(_pad_rows(b, n))
        out += [h, l, h]
    return jnp.concatenate(out, axis=0)


def _load_field(ref):
    return jnp.concatenate([ref[p] for p in range(NQ)], axis=1)


def _store_field(ref, val):
    for q in range(NQ):
        ref[q] = val[:, q * E:(q + 1) * E]


def _mix_vol(a_ref, star_ref, out_ref, sign):
    for q in range(NQ):
        acc = None
        for p in range(NQ):
            srow = star_ref[p, q]
            for d in range(3):
                t = a_ref[d * NB:(d + 1) * NB, p * E:(p + 1) * E] * srow[d:d + 1, :]
                acc = t if acc is None else acc + t
        out_ref[:, q * E:(q + 1) * E] = acc if sign > 0 else -acc


def _taylor(x, star_ref, stiff_p, d_ref, a_ref, accs):
    for ref, w in accs:
        ref[...] = w[0] * x
    d_ref[...] = x
    for k in range(ORDER - 1):
        a_ref[...] = _bdot(stiff_p, _rhs3(d_ref[...]))
        _mix_vol(a_ref, star_ref, d_ref, -1)
        dn = d_ref[...]
        for ref, w in accs:
            ref[...] = ref[...] + w[k + 1] * dn


def _table(x, trace_p, yt_ref, t_ref):
    yt = _bdot(trace_p, _rhs3(x))
    for p in range(NQ):
        yt_ref[p] = yt[:, p * E:(p + 1) * E]
    t_ref[...] = jnp.zeros(t_ref.shape, F32)
    for f in range(4):
        for p in range(NQ):
            t_ref[p * FP:p * FP + NF, f * E:(f + 1) * E] = yt_ref[p, pl.ds(f, NF, stride=4), :]


def _send(tables, send_ref, outs):
    rows = lax.broadcasted_iota(jnp.int32, (4 * E, 3 * E), 0)
    onehot = jnp.where(rows == send_ref[...].reshape(1, 3 * E), 1.0, 0.0).astype(BF)
    s = _sel(jnp.concatenate(_split3(jnp.concatenate(tables, axis=0)), axis=1), onehot)
    for i, (lo_ref, hi_ref, g_ref) in enumerate(outs):
        blk = s[i * TR:(i + 1) * TR]
        lo_ref[...] = blk[:, 0:E]
        hi_ref[...] = blk[:, E:2 * E]
        g_ref[...] = blk[:, 2 * E:3 * E]


def _gather(comb, slot_ref, face_ref, g_ref, received):
    rows = lax.broadcasted_iota(jnp.int32, (4 * E, E), 0)
    parts = jnp.concatenate(_split3(comb), axis=1)
    for f in range(4):
        v = slot_ref[f:f + 1, :]
        if received == "fault":
            s = v - E
            src = jnp.where((v < E) | ((s >= 2 * E) & (s < 2 * E + 64)), -1, s - jnp.where(s >= 2 * E, 64, 0))
            rows = lax.broadcasted_iota(jnp.int32, (3 * E, E), 0)
        elif received:
            s = v - E
            src = jnp.where(v < E, -1, s + jnp.where(s >= 2 * E, 64, 0))
        else:
            src = jnp.where(v < E, face_ref[f:f + 1, :] * E + v, -1)
        onehot = jnp.where(rows == src, 1.0, 0.0).astype(BF)
        g_ref[:, f * E:(f + 1) * E] = _sel(parts, onehot)


def _fmix(pairs, yf_ref, base_ref=None):
    for q in range(NQ):
        accs = [None] * 4
        for p in range(NQ):
            rows = [fl_ref[p, q] for _, fl_ref in pairs]
            for f in range(4):
                t = None
                for (t_ref, _), row in zip(pairs, rows):
                    u = t_ref[p * FP:(p + 1) * FP, f * E:(f + 1) * E] * row[f:f + 1, :]
                    t = u if t is None else t + u
                accs[f] = t if accs[f] is None else accs[f] + t
        for f in range(4):
            acc = accs[f]
            if base_ref is not None:
                acc = base_ref[f * FP:(f + 1) * FP, q * E:(q + 1) * E] + acc
            yf_ref[f * FP:(f + 1) * FP, q * E:(q + 1) * E] = acc


def _lift_parts(lift_ref, lt_ref):
    lt_ref[:, 0:NB] = _rows84(lift_ref)
    return _lhs3_t([lt_ref[pl.ds(f, NF, stride=4), 0:NB] for f in range(4)], 32)


def _vol(b, x, star_ref, stiff_ref, a_ref, v_ref):
    xr = _rhs3(x)
    for d in range(3):
        a_ref[d * NB:(d + 1) * NB, :] = _tdot(_lhs3_t([stiff_ref[d]], 64), xr)
    _mix_vol(a_ref, star_ref, v_ref, 1)
    return b + v_ref[...]


def _partial(b, x, own_ref, star_ref, fo_ref, fn_ref, stiff_ref, slot_ref, face_ref,
             a_ref, v_ref, g_ref, bv_ref, yp_ref):
    bv_ref[...] = _vol(b, x, star_ref, stiff_ref, a_ref, v_ref)
    _gather(own_ref[...], slot_ref, face_ref, g_ref, False)
    _fmix([(own_ref, fo_ref), (g_ref, fn_ref)], yp_ref)


def _finish(bv_ref, yp_ref, recv, fn_ref, lift_p, slot_ref, face_ref, g_ref, yf_ref, received=True):
    _gather(jnp.concatenate(recv, axis=1), slot_ref, face_ref, g_ref, received)
    _fmix([(g_ref, fn_ref)], yf_ref, yp_ref)
    ftot = _tdot(lift_p, _rhs3_rows([yf_ref[f * FP:(f + 1) * FP, :] for f in range(4)], 32))
    return bv_ref[...] - ftot


def _kernel_a1(x_ref, star_ref, stiff_ref, trace_ref, send_ref,
               first_ref, later_ref, t1_ref, s1lo, s1hi, s1g,
               d_ref, a_ref, acc1_ref, acc2_ref, yt_ref):
    x = _load_field(x_ref)
    stiff_st = jnp.concatenate([stiff_ref[d] for d in range(3)], axis=0)
    _taylor(x, star_ref, _lhs3(stiff_st), d_ref, a_ref, [(acc1_ref, W_FIRST), (acc2_ref, W_LATER)])
    first = acc1_ref[...]
    first_ref[...] = first
    later_ref[...] = acc2_ref[...]
    _table(first, _lhs3(_rows84(trace_ref)), yt_ref, t1_ref)
    _send([t1_ref[...]], send_ref, [(s1lo, s1hi, s1g)])


def _kernel_a2(grp_ref, x_ref, first_ref, later_ref, t1_ref, s1lo, s1hi, s1g, star_ref, fo_ref, fn_ref,
               stiff_ref, trace_ref, send_ref, slot_ref, face_ref,
               fl_ref, t1l_ref, plo, phi, pg, slg, bv_ref, yp_ref,
               tl_ref, yt_ref, sllo, slhi, a_ref, v_ref, g_ref):
    @pl.when(grp_ref[0] != 0)
    def _():
        later = later_ref[...]
        fl_ref[...] = first_ref[...] + later
        _table(later, _lhs3(_rows84(trace_ref)), yt_ref, tl_ref)
        t1l_ref[...] = t1_ref[...] + tl_ref[...]
        _send([tl_ref[...]], send_ref, [(sllo, slhi, slg)])
        plo[...] = s1lo[...] + sllo[...]
        phi[...] = s1hi[...] + slhi[...]
        pg[...] = s1g[...] + slg[...]

    @pl.when(grp_ref[0] == 0)
    def _():
        _partial(_load_field(x_ref), first_ref[...], t1_ref, star_ref, fo_ref, fn_ref, stiff_ref,
                 slot_ref, face_ref, a_ref, v_ref, g_ref, bv_ref, yp_ref)


def _kernel_b(grp_ref, x_ref, fl_ref, t1l_ref, s1g, plo, phi, pg, slg, bv_ref, yp_ref,
              r1lo, r1hi, r1ghi, slot_ref, face_ref, star_ref, fn_ref,
              stiff_ref, lift_ref, trace_ref, send_ref,
              base_ref, integ_ref, own_ref, elo, ehi, egup, egdn,
              d_ref, a_ref, yf_ref, g_ref, acc_ref, yt_ref, lt_ref):
    grp = grp_ref[0]

    @pl.when(grp == 0)
    def _():
        recv = [r1lo[...], r1hi[...], r1ghi[...]]
        mid = _finish(bv_ref, yp_ref, recv, fn_ref, _lift_parts(lift_ref, lt_ref), slot_ref, face_ref,
                      g_ref, yf_ref, "fault")
        base_ref[...] = mid
        stiff_st = jnp.concatenate([stiff_ref[d] for d in range(3)], axis=0)
        _taylor(mid, star_ref, _lhs3(stiff_st), d_ref, a_ref, [(acc_ref, W_FIRST)])
        second = acc_ref[...]
        integ_ref[...] = second
        _table(second, _lhs3(_rows84(trace_ref)), yt_ref, own_ref)
        _send([own_ref[...]], send_ref, [(elo, ehi, egdn)])
        egup[...] = s1g[...] + egdn[...]

    @pl.when(grp != 0)
    def _():
        base_ref[...] = _load_field(x_ref)
        integ_ref[...] = fl_ref[...]
        own_ref[...] = t1l_ref[...]
        elo[...] = plo[...]
        ehi[...] = phi[...]
        egup[...] = pg[...]

    @pl.when(grp == 1)
    def _():
        egdn[...] = slg[...]

    @pl.when(grp > 1)
    def _():
        egdn[...] = pg[...]


def _kernel_b2(base_ref, integ_ref, own_ref, star_ref, fo_ref, fn_ref, stiff_ref, slot_ref, face_ref,
               bv_ref, yp_ref, a_ref, v_ref, g_ref):
    _partial(base_ref[...], integ_ref[...], own_ref, star_ref, fo_ref, fn_ref, stiff_ref,
             slot_ref, face_ref, a_ref, v_ref, g_ref, bv_ref, yp_ref)


def _kernel_c(bv_ref, yp_ref, r2lo, r2hi, r2glo, r2ghi, slot_ref, face_ref, fn_ref, lift_ref,
              out_ref, yf_ref, g_ref, lt_ref):
    recv = [r2lo[...], r2hi[...], r2glo[...], r2ghi[...]]
    out = _finish(bv_ref, yp_ref, recv, fn_ref, _lift_parts(lift_ref, lt_ref), slot_ref, face_ref,
                  g_ref, yf_ref)
    _store_field(out_ref, out)


def _vmem():
    return pl.BlockSpec(memory_space=pltpu.VMEM)


def _smem():
    return pl.BlockSpec(memory_space=pltpu.SMEM)


def _sds(shape):
    return jax.ShapeDtypeStruct(shape, F32)


def exchange(lo, hi, gup, gdn):
    n_dom = lax.axis_size("dom")
    n_grp = lax.axis_size("grp")
    from_lo = lax.ppermute(hi, "dom", [(i, i + 1) for i in range(n_dom - 1)])
    from_hi = lax.ppermute(lo, "dom", [(i + 1, i) for i in range(n_dom - 1)])
    from_glo = lax.ppermute(gup, "grp", [(i, i + 1) for i in range(n_grp - 1)])
    from_ghi = lax.ppermute(gdn, "grp", [(i + 1, i) for i in range(n_grp - 1)])
    return from_lo, from_hi, from_glo, from_ghi


def exchange_fault(lo, hi, g):
    n_dom = lax.axis_size("dom")
    axes = ("grp", "dom")
    from_lo = lax.ppermute(hi, axes, [(i, i + 1) for i in range(n_dom - 1)])
    from_hi = lax.ppermute(lo, axes, [(i + 1, i) for i in range(n_dom - 1)])
    from_ghi = lax.ppermute(g, axes, [(n_dom + i, i) for i in range(n_dom)])
    return from_lo, from_hi, from_ghi


def local(state, star, flux_own, flux_nbr, stiff, trace, lift, nbr_slot, nbr_face, send_slot):
    grp = lax.axis_index("grp").astype(jnp.int32).reshape(1)
    x0 = jnp.transpose(state, (1, 0, 2))
    star = jnp.transpose(star, (1, 2, 0, 3))
    flux_own = jnp.transpose(flux_own, (1, 2, 0, 3))
    flux_nbr = jnp.transpose(flux_nbr, (1, 2, 0, 3))
    trace = jnp.transpose(trace, (1, 0, 2))
    lift = jnp.transpose(lift, (2, 0, 1))
    send = send_slot

    field = _sds((NQ, NB, E))
    flat = _sds((NB, LN))
    table = _sds((TR, 4 * E))
    part = _sds((TR, E))
    yflux = _sds((4 * FP, LN))
    wide = pltpu.VMEM((NB, LN), F32)
    amat = pltpu.VMEM((3 * NB, LN), F32)
    tab = pltpu.VMEM((TR, 4 * E), F32)
    ytr = pltpu.VMEM((NQ, 4 * NF, E), F32)
    yfs = pltpu.VMEM((4 * FP, LN), F32)
    lts = pltpu.VMEM((4 * NF, E), F32)

    first, later, t1, s1lo, s1hi, s1g = pl.pallas_call(
        _kernel_a1,
        out_shape=(flat, flat, table, part, part, part),
        in_specs=[_vmem()] * 5,
        out_specs=tuple([_vmem()] * 6),
        scratch_shapes=[wide, amat, wide, wide, ytr],
    )(x0, star, stiff, trace, send)

    r1 = exchange_fault(s1lo, s1hi, s1g)

    fl, t1l, plo, phi, pg, slg, bv1, yp1 = pl.pallas_call(
        _kernel_a2,
        out_shape=(flat, table, part, part, part, part, flat, yflux),
        in_specs=[_smem()] + [_vmem()] * 15,
        out_specs=tuple([_vmem()] * 8),
        scratch_shapes=[tab, ytr, pltpu.VMEM((TR, E), F32), pltpu.VMEM((TR, E), F32), amat, wide, tab],
    )(grp, x0, first, later, t1, s1lo, s1hi, s1g, star, flux_own, flux_nbr, stiff, trace, send,
      nbr_slot, nbr_face)

    base, integ, own, elo, ehi, egup, egdn = pl.pallas_call(
        _kernel_b,
        out_shape=(flat, flat, table, part, part, part, part),
        in_specs=[_smem()] + [_vmem()] * 21,
        out_specs=tuple([_vmem()] * 7),
        scratch_shapes=[wide, amat, yfs, tab, wide, ytr, lts],
    )(grp, x0, fl, t1l, s1g, plo, phi, pg, slg, bv1, yp1, *r1, nbr_slot, nbr_face, star, flux_nbr,
      stiff, lift, trace, send)

    r2 = exchange(elo, ehi, egup, egdn)

    bv2, yp2 = pl.pallas_call(
        _kernel_b2,
        out_shape=(flat, yflux),
        in_specs=[_vmem()] * 9,
        out_specs=(_vmem(), _vmem()),
        scratch_shapes=[amat, wide, tab],
    )(base, integ, own, star, flux_own, flux_nbr, stiff, nbr_slot, nbr_face)

    out = pl.pallas_call(
        _kernel_c,
        out_shape=field,
        in_specs=[_vmem()] * 10,
        out_specs=_vmem(),
        scratch_shapes=[yfs, tab, lts],
    )(bv2, yp2, *r2, nbr_slot, nbr_face, flux_nbr, lift)
    return jnp.transpose(out, (1, 0, 2))


def solution(mesh):
    in_specs = (
        P(None, None, ("grp", "dom")),
        P(None, None, None, ("grp", "dom")),
        P(None, None, None, ("grp", "dom")),
        P(None, None, None, ("grp", "dom")),
        P(),
        P(),
        P(),
        P(None, ("grp", "dom")),
        P(None, ("grp", "dom")),
        P(("grp", "dom")),
    )
    out_specs = P(None, None, ("grp", "dom"))
    return jax.shard_map(local, mesh=mesh, in_specs=in_specs, out_specs=out_specs, check_vma=False)
```
